768 devices in a mesh: pos: 64 (over x, y, core), tile: 12 (over z).
Axes of the slice: x: 4, y: 8, z: 12, core: 2. Of those that a mesh axis runs over, the one named last changes fastest.
Arguments:
- obj_tiles: bfloat16 [1536, 4, 4096], P('pos'), may hold values from -4.1875 to 4.1875
- tile_map: int32 [32, 48], replicated, may hold values from 0 to 1535, as said below
- offsets: int32 [768, 2], replicated, may hold values from 1 to 2943, as said below
- probe: float32 [2, 128, 128], replicated, may hold values from -6 to 6
- intens: float32 [768, 128, 128], P(('pos', 'tile')), may hold values from 0.05 to 2
Outputs:
- obj_grad: float32 [1536, 4, 4096], P('pos')
- probe_grad: float32 [2, 128, 128], replicated
The draws below stay inside these ranges and needn't reach their ends.
Inputs may be any that keep to these rules, and one draw needn't show every extreme that they name: tile_map holds every storage index once. A tile's owner is its storage index // 24; the owner depends only on the tile row mod 8 and the tile column mod 8, and different such classes have different owners. `offsets`: every patch lies inside the window, and neither its row nor its column offset is a multiple of 64.
All inputs are finite; a program needn't handle non-finite values.
Results may differ from the reference program's by a relative error of at most 0.0023.
Values may be sent and summed in bfloat16 or wider, within the bound.
No kernel may reach another device: no remote copies, remote signals or barrier semaphores. Data moves between devices by JAX's collectives and lax.ppermute only.
A program may use at most 32 MiB of HBM per device.

```python
import math
import jax
import jax.numpy as jnp
from jax import lax

PROBE = 128
TS = 64
SPAN = 3
OWN_R = 8
OWN_C = 8
BLK_C = 6
TILE_DEV = 24
TR = 32
TC = 48
NTILE = 1536
NPOS = 768


def draw_offsets(key, part):
    key_rows, key_cols, key_fine_r, key_fine_c = jax.random.split(key, 4)
    tile_rows = jax.random.randint(key_rows, (NPOS,), 0, TR - SPAN + 1)
    tile_cols = jax.random.randint(key_cols, (NPOS,), 0, TC - SPAN + 1)
    fine_rows = jax.random.randint(key_fine_r, (NPOS,), 1, TS)
    fine_cols = jax.random.randint(key_fine_c, (NPOS,), 1, TS)
    tile_rows = tile_rows.at[0].set(0).at[NPOS - 1].set(TR - SPAN)
    tile_cols = tile_cols.at[0].set(0).at[NPOS - 1].set(TC - SPAN)
    fine_rows = fine_rows.at[0].set(1).at[NPOS - 1].set(TS - 1)
    fine_cols = fine_cols.at[0].set(1).at[NPOS - 1].set(TS - 1)
    return jnp.stack([tile_rows * TS + fine_rows, tile_cols * TS + fine_cols], axis=1).astype(jnp.int32)


def draw_tile_map(key, part):
    key_rows, key_cols, key_slots = jax.random.split(key, 3)
    row_perm = jax.random.permutation(key_rows, OWN_R).astype(jnp.int32)
    col_perm = jax.random.permutation(key_cols, OWN_C).astype(jnp.int32)
    slot_perm = jax.random.permutation(key_slots, TILE_DEV).astype(jnp.int32)
    grid_r = jnp.arange(TR, dtype=jnp.int32)[:, None]
    grid_c = jnp.arange(TC, dtype=jnp.int32)[None, :]
    owner_id = row_perm[grid_r % OWN_R] * OWN_C + col_perm[grid_c % OWN_C]
    local_id = slot_perm[grid_r // OWN_R * BLK_C + grid_c // OWN_C]
    return (owner_id * TILE_DEV + local_id).astype(jnp.int32)


def steps_of(own_key, shape, shards, smallest, largest):
    loudness, own = 1.0, jax.random.fold_in(own_key, 6)
    for dim, shards_of in shards:
        heights = jnp.exp(jax.random.uniform(jax.random.fold_in(own, dim), (shards_of,), jnp.float32, smallest / len(shards), largest / len(shards)))
        loudness = loudness * jnp.repeat(heights, shape[dim] // shards_of).reshape([-1 if axis == dim else 1 for axis in range(len(shape))])
    return loudness


def gaussian(own_key, extent, scale, reach, cuts=(), kind=jnp.bfloat16):
    drawn = scale * jax.random.normal(own_key, extent, jnp.float32)
    if cuts:
        drawn = drawn * steps_of(own_key, extent, cuts, -0.22, 0.18)
    return jnp.clip(drawn, -reach, reach).astype(kind)


def setup_inputs(seed: int = 0) -> dict:
    key_list = jax.random.split(jax.random.key(seed), 6)
    return {
        "obj_tiles": gaussian(key_list[0], (NTILE, 4, TS * TS), 0.7, 4.1875, ((0, 64),)),
        "tile_map": draw_tile_map(jax.random.fold_in(key_list[5], 71), 0),
        "offsets": draw_offsets(jax.random.fold_in(key_list[5], 71), 0),
        "probe": gaussian(key_list[3], (2, PROBE, PROBE), 1.0, 6.0, (), jnp.float32),
        "intens": jnp.clip(jnp.exp(math.log(2.0) - 3.6888794 * jax.random.uniform(key_list[4], (NPOS, PROBE, PROBE), jnp.float32) ** steps_of(key_list[4], (NPOS, PROBE, PROBE), ((0, 768),), -0.2, 0.2)), 0.05, 2.0),
    }


def propagator_phase(width_px):
    positions = jnp.arange(width_px, dtype=jnp.int32)
    centred = (positions + width_px // 2) % width_px - width_px // 2
    square = (centred * centred).astype(jnp.float32)
    return (square[:, None] + square[None, :]) * (-0.2 / width_px)


def forward_ft(field):
    return jnp.fft.fft2(field, norm="ortho")


def inverse_ft(field):
    return jnp.fft.ifft2(field, norm="ortho")


def reference(obj_tiles, tile_map, offsets, probe, intens):
    grid_rows, grid_cols = tile_map.shape
    n_comps = obj_tiles.shape[1]
    arranged = obj_tiles[tile_map.reshape(-1)].astype(jnp.float32)
    window_img = arranged.reshape(grid_rows, grid_cols, n_comps, TS, TS).transpose(2, 0, 3, 1, 4).reshape(n_comps, grid_rows * TS, grid_cols * TS)
    angles = propagator_phase(PROBE)
    kernel = lax.complex(jnp.cos(angles), jnp.sin(angles))
    probe_c = lax.complex(probe[0], probe[1])
    zero_idx = jnp.zeros((), jnp.int32)

    def accumulate(position, state_pair):
        grad_img, probe_acc = state_pair
        corner = offsets[position].astype(jnp.int32)
        start_at = (zero_idx, corner[0], corner[1])
        patch_px = lax.dynamic_slice(window_img, start_at, (n_comps, PROBE, PROBE))
        entry_wave = lax.complex(patch_px[0], patch_px[1])
        exit_wave = lax.complex(patch_px[2], patch_px[3])
        spread = inverse_ft(kernel * forward_ft(probe_c * entry_wave))
        far_field = forward_ft(spread * exit_wave)
        excess = far_field.real * far_field.real + far_field.imag * far_field.imag - intens[position]
        back_wave = inverse_ft(excess * far_field)
        grad_exit = jnp.conj(spread) * back_wave
        inner_wave = inverse_ft(jnp.conj(kernel) * forward_ft(jnp.conj(exit_wave) * back_wave))
        grad_entry = jnp.conj(probe_c) * inner_wave
        grad_probe = jnp.conj(entry_wave) * inner_wave
        rounded = jnp.stack([grad_entry.real, grad_entry.imag, grad_exit.real, grad_exit.imag]).astype(jnp.bfloat16)
        rounded = lax.optimization_barrier(rounded).astype(jnp.float32)
        current = lax.dynamic_slice(grad_img, start_at, (n_comps, PROBE, PROBE))
        grad_img = lax.dynamic_update_slice(grad_img, current + rounded, start_at)
        probe_acc = probe_acc + jnp.stack([grad_probe.real, grad_probe.imag])
        return grad_img, probe_acc

    grad_init = jnp.zeros(window_img.shape, jnp.float32)
    probe_init = jnp.zeros((2, PROBE, PROBE), jnp.float32)
    grad_img, probe_acc = lax.fori_loop(0, NPOS, accumulate, (grad_init, probe_init))
    blocks = grad_img.reshape(n_comps, grid_rows, TS, grid_cols, TS).transpose(1, 3, 0, 2, 4).reshape(grid_rows * grid_cols, n_comps, TS * TS)
    obj_grad = jnp.zeros_like(blocks).at[tile_map.reshape(-1)].set(blocks)
    return obj_grad, probe_acc
```

```python
import math

import jax
import jax.numpy as jnp
from jax import lax
from jax.sharding import PartitionSpec as P

TS = 64
OWN_R = 8


def matmul_hi(left_op, right_op):
    return jnp.dot(
        left_op, right_op, precision=lax.Precision.HIGHEST, preferred_element_type=jnp.float32
    )


def spectral_tables(width_px):
    positions = jnp.arange(width_px, dtype=jnp.int32)
    phase_idx = positions[:, None] * positions[None, :] % width_px
    angles = phase_idx.astype(jnp.float32) * (2.0 * math.pi / width_px)
    norm_factor = 1.0 / math.sqrt(width_px)
    return (jnp.cos(angles) * norm_factor, -jnp.sin(angles) * norm_factor)


def complex_matmul(left_re, left_im, right_re, right_im):
    out_re = matmul_hi(left_re, right_re) - matmul_hi(left_im, right_im)
    out_im = matmul_hi(left_re, right_im) + matmul_hi(left_im, right_re)
    return (out_re, out_im)


def propagation_matrix(width_px, fwd_re, fwd_im, sign_val):
    positions = jnp.arange(width_px, dtype=jnp.int32)
    centred = (positions + width_px // 2) % width_px - width_px // 2
    angles = (centred * centred).astype(jnp.float32) * (-0.2 / width_px) * sign_val
    phase_re = jnp.cos(angles)[:, None]
    phase_im = jnp.sin(angles)[:, None]
    scaled_re = phase_re * fwd_re - phase_im * fwd_im
    scaled_im = phase_re * fwd_im + phase_im * fwd_re
    return complex_matmul(fwd_re, -fwd_im, scaled_re, scaled_im)


def transform(part_re, part_im, table_re, table_im):
    mid_re, mid_im = complex_matmul(part_re, part_im, table_re, table_im)
    return complex_matmul(table_re, table_im, mid_re, mid_im)


def product(left_re, left_im, right_re, right_im):
    return (left_re * right_re - left_im * right_im, left_re * right_im + left_im * right_re)


def one_hot(index, size, live=None):
    hit = index[:, None] == jnp.arange(size, dtype=index.dtype)[None, :]
    if live is not None:
        hit = hit & live[:, None]
    return hit.astype(jnp.bfloat16)


def per_device(obj_tiles, tile_map, offsets, probe, intens):
    owners = lax.axis_size("pos")
    layers = lax.axis_size("tile")
    me_pos = lax.axis_index("pos")
    me_tile = lax.axis_index("tile")
    tiles_dev = obj_tiles.shape[0]
    n_comps = obj_tiles.shape[1]
    tile_edge = TS
    width_px = probe.shape[-1]
    tile_span = width_px // tile_edge + 1
    own_c = owners // OWN_R
    grid_r, grid_c = tile_map.shape
    span_idx = jnp.arange(tile_span, dtype=jnp.int32)

    mine = (tile_map // tiles_dev) == me_pos
    class_r = jnp.sum(jnp.where(jnp.any(mine[:OWN_R], axis=1), jnp.arange(OWN_R), 0))
    class_c = jnp.sum(jnp.where(jnp.any(mine[:, :own_c], axis=0), jnp.arange(own_c), 0))
    blocks = tile_map.reshape(grid_r // OWN_R, OWN_R, grid_c // own_c, own_c)
    my_blocks = lax.dynamic_index_in_dim(blocks, class_r, 1, keepdims=False)
    my_blocks = lax.dynamic_index_in_dim(my_blocks, class_c, 2, keepdims=False)
    my_blocks = my_blocks - me_pos * tiles_dev

    by_device = offsets.reshape(owners, layers, 2)
    peer_corners = lax.dynamic_index_in_dim(by_device, me_tile, 1, keepdims=False)
    peer_r = peer_corners[:, 0] // tile_edge
    peer_c = peer_corners[:, 1] // tile_edge
    step_r = (class_r - peer_r) % OWN_R
    step_c = (class_c - peer_c) % own_c
    send_live = (step_r < tile_span) & (step_c < tile_span)
    hit_r = (peer_r + jnp.minimum(step_r, tile_span - 1)) // OWN_R
    hit_c = (peer_c + jnp.minimum(step_c, tile_span - 1)) // own_c
    send_local = my_blocks.reshape(-1)[hit_r * (grid_c // own_c) + hit_c]
    send_sel = one_hot(send_local, tiles_dev, send_live)
    chosen = obj_tiles[send_local]

    my_corner = lax.dynamic_index_in_dim(offsets, me_pos * layers + me_tile, 0, keepdims=False)
    row_ids = my_corner[0] // tile_edge + span_idx
    col_ids = my_corner[1] // tile_edge + span_idx
    my_owner = (tile_map[row_ids[:, None], col_ids[None, :]] // tiles_dev).reshape(-1)
    inner_y = my_corner[0] % tile_edge
    inner_x = my_corner[1] % tile_edge
    zero_idx = jnp.zeros((), jnp.int32)
    fwd_re, fwd_im = spectral_tables(width_px)
    ahead_re, ahead_im = propagation_matrix(width_px, fwd_re, fwd_im, 1.0)
    behind_re, behind_im = propagation_matrix(width_px, fwd_re, fwd_im, -1.0)
    probe_re = probe[0]
    probe_im = probe[1]
    received = lax.all_to_all(chosen, "pos", split_axis=0, concat_axis=0, tiled=True)
    pieces = received[my_owner]
    region = pieces.reshape(tile_span, tile_span, n_comps, tile_edge, tile_edge).transpose(
        2, 0, 3, 1, 4
    )
    region = region.reshape(n_comps, tile_span * tile_edge, tile_span * tile_edge)
    patch_px = lax.dynamic_slice(
        region, (zero_idx, inner_y, inner_x), (n_comps, width_px, width_px)
    )
    fetched = patch_px.astype(jnp.float32)
    entry_patch = fetched[:2]
    leaving = fetched[2:]
    first_re, first_im = product(probe_re, probe_im, entry_patch[0], entry_patch[1])
    spread_re, spread_im = transform(first_re, first_im, ahead_re, ahead_im)
    second_re, second_im = product(spread_re, spread_im, leaving[0], leaving[1])
    far_re, far_im = transform(second_re, second_im, fwd_re, fwd_im)
    excess = far_re * far_re + far_im * far_im - intens[0]
    back_re, back_im = transform(excess * far_re, excess * far_im, fwd_re, -fwd_im)
    exit_re, exit_im = product(spread_re, -spread_im, back_re, back_im)
    mid_re, mid_im = product(leaving[0], -leaving[1], back_re, back_im)
    inner_re, inner_im = transform(mid_re, mid_im, behind_re, behind_im)
    entry_re, entry_im = product(probe_re, -probe_im, inner_re, inner_im)
    grad_re, grad_im = product(entry_patch[0], -entry_patch[1], inner_re, inner_im)
    patch_grad = jnp.stack([entry_re, entry_im, exit_re, exit_im]).astype(jnp.bfloat16)

    region_px = tile_span * tile_edge
    shift_y = one_hot(jnp.arange(region_px, dtype=jnp.int32) - inner_y, width_px)
    shift_x = one_hot(jnp.arange(region_px, dtype=jnp.int32) - inner_x, width_px)
    shift_y = shift_y.reshape(tile_span, tile_edge, width_px)
    shift_x = shift_x.reshape(tile_span, tile_edge, width_px)
    rows_cut = jnp.einsum("irk,ckm->cirm", shift_y, patch_grad, preferred_element_type=jnp.float32)
    rows_cut = rows_cut.astype(jnp.bfloat16)
    tiles_cut = jnp.einsum("cirm,jsm->ijcrs", rows_cut, shift_x, preferred_element_type=jnp.float32)
    tiles_cut = tiles_cut.astype(jnp.bfloat16).reshape(
        tile_span * tile_span, n_comps, tile_edge * tile_edge
    )
    slot_of = jnp.sum(
        jnp.where(my_owner[None, :] == jnp.arange(owners)[:, None], jnp.arange(my_owner.size), 0),
        axis=1,
    )
    outgoing = tiles_cut[slot_of]
    returned = lax.all_to_all(outgoing, "pos", split_axis=0, concat_axis=0, tiled=True)
    local_sum = jnp.einsum("nk,ncp->kcp", send_sel, returned, preferred_element_type=jnp.float32)
    probe_part = jnp.stack([grad_re, grad_im])
    tile_total = lax.psum(local_sum, "tile")
    probe_total = reduce_probe(probe_part, owners, layers)
    return (tile_total, probe_total)


def reduce_probe(probe_part, owners, layers):
    piece_len = probe_part.size // owners
    pieces = probe_part.reshape(owners, piece_len)
    mine = jnp.sum(lax.all_to_all(pieces, "pos", 0, 0, tiled=True), axis=0)
    spread = jnp.broadcast_to(mine[None], (layers, piece_len))
    mine = jnp.sum(lax.all_to_all(spread, "tile", 0, 0, tiled=True), axis=0)
    spread = jnp.broadcast_to(mine[None], (owners, piece_len))
    gathered = lax.all_to_all(spread, "pos", 0, 0, tiled=True)
    return gathered.reshape(probe_part.shape)


def solution(mesh):
    in_specs = (P("pos", None, None), P(), P(), P(), P(("pos", "tile"), None, None))
    out_specs = (P("pos", None, None), P())
    return jax.shard_map(
        per_device, mesh=mesh, in_specs=in_specs, out_specs=out_specs, check_vma=False
    )
```

```python
import math

import jax
import jax.numpy as jnp
from jax import lax
from jax.sharding import PartitionSpec as P

TS = 64
OWN_R = 8


def matmul_hi(left_op, right_op):
    return jnp.dot(
        left_op, right_op, precision=lax.Precision.HIGHEST, preferred_element_type=jnp.float32
    )


def spectral_tables(width_px):
    positions = jnp.arange(width_px, dtype=jnp.int32)
    phase_idx = positions[:, None] * positions[None, :] % width_px
    angles = phase_idx.astype(jnp.float32) * (2.0 * math.pi / width_px)
    norm_factor = 1.0 / math.sqrt(width_px)
    return (jnp.cos(angles) * norm_factor, -jnp.sin(angles) * norm_factor)


def complex_matmul(left_re, left_im, right_re, right_im):
    out_re = matmul_hi(left_re, right_re) - matmul_hi(left_im, right_im)
    out_im = matmul_hi(left_re, right_im) + matmul_hi(left_im, right_re)
    return (out_re, out_im)


def propagation_matrix(width_px, fwd_re, fwd_im, sign_val):
    positions = jnp.arange(width_px, dtype=jnp.int32)
    centred = (positions + width_px // 2) % width_px - width_px // 2
    angles = (centred * centred).astype(jnp.float32) * (-0.2 / width_px) * sign_val
    phase_re = jnp.cos(angles)[:, None]
    phase_im = jnp.sin(angles)[:, None]
    scaled_re = phase_re * fwd_re - phase_im * fwd_im
    scaled_im = phase_re * fwd_im + phase_im * fwd_re
    return complex_matmul(fwd_re, -fwd_im, scaled_re, scaled_im)


def transform(part_re, part_im, table_re, table_im):
    mid_re, mid_im = complex_matmul(part_re, part_im, table_re, table_im)
    return complex_matmul(table_re, table_im, mid_re, mid_im)


def product(left_re, left_im, right_re, right_im):
    return (left_re * right_re - left_im * right_im, left_re * right_im + left_im * right_re)


def one_hot(index, size, live=None):
    hit = index[:, None] == jnp.arange(size, dtype=index.dtype)[None, :]
    if live is not None:
        hit = hit & live[:, None]
    return hit.astype(jnp.bfloat16)


def per_device(obj_tiles, tile_map, offsets, probe, intens):
    owners = lax.axis_size("pos")
    layers = lax.axis_size("tile")
    me_pos = lax.axis_index("pos")
    me_tile = lax.axis_index("tile")
    tiles_dev = obj_tiles.shape[0]
    n_comps = obj_tiles.shape[1]
    tile_edge = TS
    width_px = probe.shape[-1]
    tile_span = width_px // tile_edge + 1
    own_c = owners // OWN_R
    grid_r, grid_c = tile_map.shape
    span_idx = jnp.arange(tile_span, dtype=jnp.int32)

    mine = (tile_map // tiles_dev) == me_pos
    local_plus = jnp.where(mine, tile_map - me_pos * tiles_dev + 1, 0).astype(jnp.bfloat16)
    by_device = offsets.reshape(owners, layers, 2)
    peer_corners = lax.dynamic_index_in_dim(by_device, me_tile, 1, keepdims=False)
    peer_r = peer_corners[:, 0:1] // tile_edge
    peer_c = peer_corners[:, 1:2] // tile_edge
    grid_rows = jnp.arange(grid_r, dtype=jnp.int32)[None, :]
    grid_cols = jnp.arange(grid_c, dtype=jnp.int32)[None, :]
    row_in = ((grid_rows >= peer_r) & (grid_rows < peer_r + tile_span)).astype(jnp.bfloat16)
    col_in = ((grid_cols >= peer_c) & (grid_cols < peer_c + tile_span)).astype(jnp.float32)
    by_col = jnp.dot(row_in, local_plus, preferred_element_type=jnp.float32)
    found = jnp.sum(by_col * col_in, axis=1).astype(jnp.int32)
    send_live = found > 0
    send_local = jnp.maximum(found - 1, 0)
    chosen = obj_tiles[send_local]

    my_corner = lax.dynamic_index_in_dim(offsets, me_pos * layers + me_tile, 0, keepdims=False)
    row_ids = my_corner[0] // tile_edge + span_idx
    col_ids = my_corner[1] // tile_edge + span_idx
    my_owner = (tile_map[row_ids[:, None], col_ids[None, :]] // tiles_dev).reshape(-1)
    inner_y = my_corner[0] % tile_edge
    inner_x = my_corner[1] % tile_edge
    zero_idx = jnp.zeros((), jnp.int32)
    fwd_re, fwd_im = spectral_tables(width_px)
    ahead_re, ahead_im = propagation_matrix(width_px, fwd_re, fwd_im, 1.0)
    behind_re, behind_im = propagation_matrix(width_px, fwd_re, fwd_im, -1.0)
    probe_re = probe[0]
    probe_im = probe[1]
    received = lax.all_to_all(chosen, "pos", split_axis=0, concat_axis=0, tiled=True)
    pieces = received[my_owner]
    region = pieces.reshape(tile_span, tile_span, n_comps, tile_edge, tile_edge).transpose(
        2, 0, 3, 1, 4
    )
    region = region.reshape(n_comps, tile_span * tile_edge, tile_span * tile_edge)
    patch_px = lax.dynamic_slice(
        region, (zero_idx, inner_y, inner_x), (n_comps, width_px, width_px)
    )
    fetched = patch_px.astype(jnp.float32)
    entry_patch = fetched[:2]
    leaving = fetched[2:]
    first_re, first_im = product(probe_re, probe_im, entry_patch[0], entry_patch[1])
    spread_re, spread_im = transform(first_re, first_im, ahead_re, ahead_im)
    second_re, second_im = product(spread_re, spread_im, leaving[0], leaving[1])
    far_re, far_im = transform(second_re, second_im, fwd_re, fwd_im)
    excess = far_re * far_re + far_im * far_im - intens[0]
    back_re, back_im = transform(excess * far_re, excess * far_im, fwd_re, -fwd_im)
    exit_re, exit_im = product(spread_re, -spread_im, back_re, back_im)
    mid_re, mid_im = product(leaving[0], -leaving[1], back_re, back_im)
    inner_re, inner_im = transform(mid_re, mid_im, behind_re, behind_im)
    entry_re, entry_im = product(probe_re, -probe_im, inner_re, inner_im)
    grad_re, grad_im = product(entry_patch[0], -entry_patch[1], inner_re, inner_im)
    patch_grad = jnp.stack([entry_re, entry_im, exit_re, exit_im]).astype(jnp.bfloat16)

    region_px = tile_span * tile_edge
    shift_y = one_hot(jnp.arange(region_px, dtype=jnp.int32) - inner_y, width_px)
    shift_x = one_hot(jnp.arange(region_px, dtype=jnp.int32) - inner_x, width_px)
    shift_y = shift_y.reshape(tile_span, tile_edge, width_px)
    shift_x = shift_x.reshape(tile_span, tile_edge, width_px)
    rows_cut = jnp.einsum("irk,ckm->cirm", shift_y, patch_grad, preferred_element_type=jnp.float32)
    rows_cut = rows_cut.astype(jnp.bfloat16)
    tiles_cut = jnp.einsum("cirm,jsm->ijcrs", rows_cut, shift_x, preferred_element_type=jnp.float32)
    tiles_cut = tiles_cut.astype(jnp.bfloat16).reshape(
        tile_span * tile_span, n_comps, tile_edge * tile_edge
    )
    slot_of = jnp.sum(
        jnp.where(my_owner[None, :] == jnp.arange(owners)[:, None], jnp.arange(my_owner.size), 0),
        axis=1,
    )
    outgoing = tiles_cut[slot_of]
    returned = lax.all_to_all(outgoing, "pos", split_axis=0, concat_axis=0, tiled=True)
    selector = one_hot(send_local, tiles_dev, send_live).T
    local_sum = jnp.dot(
        selector,
        returned.reshape(owners, n_comps * tile_edge * tile_edge),
        preferred_element_type=jnp.float32,
    )
    probe_part = jnp.stack([grad_re, grad_im])
    tile_total = lax.psum(local_sum, "tile")
    probe_total = reduce_probe(probe_part, owners, layers)
    return (tile_total.reshape(tiles_dev, n_comps, tile_edge * tile_edge), probe_total)


def reduce_probe(probe_part, owners, layers):
    piece_len = probe_part.size // owners
    pieces = probe_part.reshape(owners, piece_len)
    mine = jnp.sum(lax.all_to_all(pieces, "pos", 0, 0, tiled=True), axis=0)
    spread = jnp.broadcast_to(mine[None], (layers, piece_len))
    mine = jnp.sum(lax.all_to_all(spread, "tile", 0, 0, tiled=True), axis=0)
    spread = jnp.broadcast_to(mine[None], (owners, piece_len))
    gathered = lax.all_to_all(spread, "pos", 0, 0, tiled=True)
    return gathered.reshape(probe_part.shape)


def solution(mesh):
    in_specs = (P("pos", None, None), P(), P(), P(), P(("pos", "tile"), None, None))
    out_specs = (P("pos", None, None), P())
    return jax.shard_map(
        per_device, mesh=mesh, in_specs=in_specs, out_specs=out_specs, check_vma=False
    )
```

```python
import math

import jax
import jax.numpy as jnp
from jax import lax
from jax.sharding import PartitionSpec as P

TS = 64
OWN_R = 8


def matmul_hi(left_op, right_op):
    return jnp.dot(
        left_op, right_op, precision=lax.Precision.HIGHEST, preferred_element_type=jnp.float32
    )


def spectral_tables(width_px):
    positions = jnp.arange(width_px, dtype=jnp.int32)
    phase_idx = positions[:, None] * positions[None, :] % width_px
    angles = phase_idx.astype(jnp.float32) * (2.0 * math.pi / width_px)
    norm_factor = 1.0 / math.sqrt(width_px)
    return (jnp.cos(angles) * norm_factor, -jnp.sin(angles) * norm_factor)


def complex_matmul(left_re, left_im, right_re, right_im):
    out_re = matmul_hi(left_re, right_re) - matmul_hi(left_im, right_im)
    out_im = matmul_hi(left_re, right_im) + matmul_hi(left_im, right_re)
    return (out_re, out_im)


def propagation_matrix(width_px, fwd_re, fwd_im, sign_val):
    positions = jnp.arange(width_px, dtype=jnp.int32)
    centred = (positions + width_px // 2) % width_px - width_px // 2
    angles = (centred * centred).astype(jnp.float32) * (-0.2 / width_px) * sign_val
    phase_re = jnp.cos(angles)[:, None]
    phase_im = jnp.sin(angles)[:, None]
    scaled_re = phase_re * fwd_re - phase_im * fwd_im
    scaled_im = phase_re * fwd_im + phase_im * fwd_re
    return complex_matmul(fwd_re, -fwd_im, scaled_re, scaled_im)


def stacked_table(table_re, table_im):
    column = jnp.concatenate([table_re, table_im], axis=0)
    block = jnp.concatenate(
        [jnp.concatenate([table_re, -table_im], axis=1), jnp.concatenate([table_im, table_re], axis=1)],
        axis=0,
    )
    return column, block


def transform(part_re, part_im, table):
    column, block = table
    left = jnp.concatenate(
        [jnp.concatenate([part_re, -part_im], axis=1), jnp.concatenate([part_im, part_re], axis=1)],
        axis=0,
    )
    mid = matmul_hi(left, column)
    out = matmul_hi(block, mid)
    width = part_re.shape[0]
    return out[:width], out[width:]


def product(left_re, left_im, right_re, right_im):
    return (left_re * right_re - left_im * right_im, left_re * right_im + left_im * right_re)


def one_hot(index, size, live=None):
    hit = index[:, None] == jnp.arange(size, dtype=index.dtype)[None, :]
    if live is not None:
        hit = hit & live[:, None]
    return hit.astype(jnp.bfloat16)


def per_device(obj_tiles, tile_map, offsets, probe, intens):
    owners = lax.axis_size("pos")
    layers = lax.axis_size("tile")
    me_pos = lax.axis_index("pos")
    me_tile = lax.axis_index("tile")
    tiles_dev = obj_tiles.shape[0]
    n_comps = obj_tiles.shape[1]
    tile_edge = TS
    width_px = probe.shape[-1]
    tile_span = width_px // tile_edge + 1
    own_c = owners // OWN_R
    grid_r, grid_c = tile_map.shape
    span_idx = jnp.arange(tile_span, dtype=jnp.int32)

    mine = (tile_map // tiles_dev) == me_pos
    local_plus = jnp.where(mine, tile_map - me_pos * tiles_dev + 1, 0).astype(jnp.bfloat16)
    by_device = offsets.reshape(owners, layers, 2)
    peer_corners = lax.dynamic_index_in_dim(by_device, me_tile, 1, keepdims=False)
    peer_r = peer_corners[:, 0:1] // tile_edge
    peer_c = peer_corners[:, 1:2] // tile_edge
    grid_rows = jnp.arange(grid_r, dtype=jnp.int32)[None, :]
    grid_cols = jnp.arange(grid_c, dtype=jnp.int32)[None, :]
    row_in = ((grid_rows >= peer_r) & (grid_rows < peer_r + tile_span)).astype(jnp.bfloat16)
    col_in = ((grid_cols >= peer_c) & (grid_cols < peer_c + tile_span)).astype(jnp.float32)
    by_col = jnp.dot(row_in, local_plus, preferred_element_type=jnp.float32)
    found = jnp.sum(by_col * col_in, axis=1).astype(jnp.int32)
    send_live = found > 0
    send_local = jnp.maximum(found - 1, 0)
    chosen = obj_tiles[send_local]

    my_corner = lax.dynamic_index_in_dim(offsets, me_pos * layers + me_tile, 0, keepdims=False)
    row_ids = my_corner[0] // tile_edge + span_idx
    col_ids = my_corner[1] // tile_edge + span_idx
    my_owner = (tile_map[row_ids[:, None], col_ids[None, :]] // tiles_dev).reshape(-1)
    inner_y = my_corner[0] % tile_edge
    inner_x = my_corner[1] % tile_edge
    zero_idx = jnp.zeros((), jnp.int32)
    fwd_re, fwd_im = spectral_tables(width_px)
    ahead_re, ahead_im = propagation_matrix(width_px, fwd_re, fwd_im, 1.0)
    behind_re, behind_im = propagation_matrix(width_px, fwd_re, fwd_im, -1.0)
    ahead = stacked_table(ahead_re, ahead_im)
    forward = stacked_table(fwd_re, fwd_im)
    backward = stacked_table(fwd_re, -fwd_im)
    behind = stacked_table(behind_re, behind_im)
    probe_re = probe[0]
    probe_im = probe[1]
    received = lax.all_to_all(chosen, "pos", split_axis=0, concat_axis=0, tiled=True)
    pieces = received[my_owner]
    region = pieces.reshape(tile_span, tile_span, n_comps, tile_edge, tile_edge).transpose(
        2, 0, 3, 1, 4
    )
    region = region.reshape(n_comps, tile_span * tile_edge, tile_span * tile_edge)
    patch_px = lax.dynamic_slice(
        region, (zero_idx, inner_y, inner_x), (n_comps, width_px, width_px)
    )
    fetched = patch_px.astype(jnp.float32)
    entry_patch = fetched[:2]
    leaving = fetched[2:]
    first_re, first_im = product(probe_re, probe_im, entry_patch[0], entry_patch[1])
    spread_re, spread_im = transform(first_re, first_im, ahead)
    second_re, second_im = product(spread_re, spread_im, leaving[0], leaving[1])
    far_re, far_im = transform(second_re, second_im, forward)
    excess = far_re * far_re + far_im * far_im - intens[0]
    back_re, back_im = transform(excess * far_re, excess * far_im, backward)
    exit_re, exit_im = product(spread_re, -spread_im, back_re, back_im)
    mid_re, mid_im = product(leaving[0], -leaving[1], back_re, back_im)
    inner_re, inner_im = transform(mid_re, mid_im, behind)
    entry_re, entry_im = product(probe_re, -probe_im, inner_re, inner_im)
    grad_re, grad_im = product(entry_patch[0], -entry_patch[1], inner_re, inner_im)
    patch_grad = jnp.stack([entry_re, entry_im, exit_re, exit_im]).astype(jnp.bfloat16)

    region_px = tile_span * tile_edge
    shift_y = one_hot(jnp.arange(region_px, dtype=jnp.int32) - inner_y, width_px)
    shift_x = one_hot(jnp.arange(region_px, dtype=jnp.int32) - inner_x, width_px)
    shift_y = shift_y.reshape(tile_span, tile_edge, width_px)
    shift_x = shift_x.reshape(tile_span, tile_edge, width_px)
    rows_cut = jnp.einsum("irk,ckm->cirm", shift_y, patch_grad, preferred_element_type=jnp.float32)
    rows_cut = rows_cut.astype(jnp.bfloat16)
    tiles_cut = jnp.einsum("cirm,jsm->ijcrs", rows_cut, shift_x, preferred_element_type=jnp.float32)
    tiles_cut = tiles_cut.astype(jnp.bfloat16).reshape(
        tile_span * tile_span, n_comps, tile_edge * tile_edge
    )
    outgoing = jnp.zeros((owners, n_comps, tile_edge * tile_edge), jnp.bfloat16).at[my_owner].set(
        tiles_cut
    )
    returned = lax.all_to_all(outgoing, "pos", split_axis=0, concat_axis=0, tiled=True)
    selector = one_hot(send_local, tiles_dev, send_live).T
    local_sum = jnp.dot(
        selector,
        returned.reshape(owners, n_comps * tile_edge * tile_edge),
        preferred_element_type=jnp.float32,
    )
    probe_part = jnp.stack([grad_re, grad_im])
    tile_total = lax.psum(local_sum, "tile")
    probe_total = reduce_probe(probe_part, owners, layers)
    return (tile_total.reshape(tiles_dev, n_comps, tile_edge * tile_edge), probe_total)


def reduce_probe(probe_part, owners, layers):
    piece_len = probe_part.size // owners
    pieces = probe_part.reshape(owners, piece_len)
    mine = jnp.sum(lax.all_to_all(pieces, "pos", 0, 0, tiled=True), axis=0)
    spread = jnp.broadcast_to(mine[None], (layers, piece_len))
    mine = jnp.sum(lax.all_to_all(spread, "tile", 0, 0, tiled=True), axis=0)
    spread = jnp.broadcast_to(mine[None], (owners, piece_len))
    gathered = lax.all_to_all(spread, "pos", 0, 0, tiled=True)
    return gathered.reshape(probe_part.shape)


def solution(mesh):
    in_specs = (P("pos", None, None), P(), P(), P(), P(("pos", "tile"), None, None))
    out_specs = (P("pos", None, None), P())
    return jax.shard_map(
        per_device, mesh=mesh, in_specs=in_specs, out_specs=out_specs, check_vma=False
    )
```

```python
import math

import jax
import jax.numpy as jnp
from jax import lax
from jax.sharding import PartitionSpec as P

TS = 64
OWN_R = 8


def matmul_hi(left_op, right_op):
    return jnp.dot(
        left_op, right_op, precision=lax.Precision.HIGHEST, preferred_element_type=jnp.float32
    )


def spectral_tables(width_px):
    positions = jnp.arange(width_px, dtype=jnp.int32)
    phase_idx = positions[:, None] * positions[None, :] % width_px
    angles = phase_idx.astype(jnp.float32) * (2.0 * math.pi / width_px)
    norm_factor = 1.0 / math.sqrt(width_px)
    return (jnp.cos(angles) * norm_factor, -jnp.sin(angles) * norm_factor)


def complex_matmul(left_re, left_im, right_re, right_im):
    out_re = matmul_hi(left_re, right_re) - matmul_hi(left_im, right_im)
    out_im = matmul_hi(left_re, right_im) + matmul_hi(left_im, right_re)
    return (out_re, out_im)


def propagation_matrix(width_px, fwd_re, fwd_im, sign_val):
    positions = jnp.arange(width_px, dtype=jnp.int32)
    centred = (positions + width_px // 2) % width_px - width_px // 2
    angles = (centred * centred).astype(jnp.float32) * (-0.2 / width_px) * sign_val
    phase_re = jnp.cos(angles)[:, None]
    phase_im = jnp.sin(angles)[:, None]
    scaled_re = phase_re * fwd_re - phase_im * fwd_im
    scaled_im = phase_re * fwd_im + phase_im * fwd_re
    return complex_matmul(fwd_re, -fwd_im, scaled_re, scaled_im)


def stacked_table(table_re, table_im):
    column = jnp.concatenate([table_re, table_im], axis=0)
    block = jnp.concatenate(
        [jnp.concatenate([table_re, -table_im], axis=1), jnp.concatenate([table_im, table_re], axis=1)],
        axis=0,
    )
    return column, block


def transform(part_re, part_im, table):
    column, block = table
    left = jnp.concatenate(
        [jnp.concatenate([part_re, -part_im], axis=1), jnp.concatenate([part_im, part_re], axis=1)],
        axis=0,
    )
    mid = matmul_hi(left, column)
    out = matmul_hi(block, mid)
    width = part_re.shape[0]
    return out[:width], out[width:]


def product(left_re, left_im, right_re, right_im):
    return (left_re * right_re - left_im * right_im, left_re * right_im + left_im * right_re)


def one_hot(index, size, live=None):
    hit = index[:, None] == jnp.arange(size, dtype=index.dtype)[None, :]
    if live is not None:
        hit = hit & live[:, None]
    return hit.astype(jnp.bfloat16)


def per_device(obj_tiles, tile_map, offsets, probe, intens):
    owners = lax.axis_size("pos")
    layers = lax.axis_size("tile")
    me_pos = lax.axis_index("pos")
    me_tile = lax.axis_index("tile")
    tiles_dev = obj_tiles.shape[0]
    n_comps = obj_tiles.shape[1]
    tile_edge = TS
    width_px = probe.shape[-1]
    tile_span = width_px // tile_edge + 1
    own_c = owners // OWN_R
    grid_r, grid_c = tile_map.shape
    span_idx = jnp.arange(tile_span, dtype=jnp.int32)

    mine = (tile_map // tiles_dev) == me_pos
    local_plus = jnp.where(mine, tile_map - me_pos * tiles_dev + 1, 0).astype(jnp.bfloat16)
    by_device = offsets.reshape(owners, layers, 2)
    peer_corners = lax.dynamic_index_in_dim(by_device, me_tile, 1, keepdims=False)
    peer_r = peer_corners[:, 0:1] // tile_edge
    peer_c = peer_corners[:, 1:2] // tile_edge
    grid_rows = jnp.arange(grid_r, dtype=jnp.int32)[None, :]
    grid_cols = jnp.arange(grid_c, dtype=jnp.int32)[None, :]
    row_in = ((grid_rows >= peer_r) & (grid_rows < peer_r + tile_span)).astype(jnp.bfloat16)
    col_in = ((grid_cols >= peer_c) & (grid_cols < peer_c + tile_span)).astype(jnp.float32)
    by_col = jnp.dot(row_in, local_plus, preferred_element_type=jnp.float32)
    found = jnp.sum(by_col * col_in, axis=1).astype(jnp.int32)
    send_live = found > 0
    send_local = jnp.maximum(found - 1, 0)
    chosen = obj_tiles[send_local]

    my_corner = lax.dynamic_index_in_dim(offsets, me_pos * layers + me_tile, 0, keepdims=False)
    row_ids = my_corner[0] // tile_edge + span_idx
    col_ids = my_corner[1] // tile_edge + span_idx
    my_owner = (tile_map[row_ids[:, None], col_ids[None, :]] // tiles_dev).reshape(-1)
    inner_y = my_corner[0] % tile_edge
    inner_x = my_corner[1] % tile_edge
    zero_idx = jnp.zeros((), jnp.int32)
    fwd_re, fwd_im = spectral_tables(width_px)
    ahead_re, ahead_im = propagation_matrix(width_px, fwd_re, fwd_im, 1.0)
    behind_re, behind_im = propagation_matrix(width_px, fwd_re, fwd_im, -1.0)
    ahead = stacked_table(ahead_re, ahead_im)
    forward = stacked_table(fwd_re, fwd_im)
    backward = stacked_table(fwd_re, -fwd_im)
    behind = stacked_table(behind_re, behind_im)
    probe_re = probe[0]
    probe_im = probe[1]
    received = lax.all_to_all(chosen, "pos", split_axis=0, concat_axis=0, tiled=True)
    pieces = received[my_owner]
    region = pieces.reshape(tile_span, tile_span, n_comps, tile_edge, tile_edge).transpose(
        2, 0, 3, 1, 4
    )
    region = region.reshape(n_comps, tile_span * tile_edge, tile_span * tile_edge)
    patch_px = lax.dynamic_slice(
        region, (zero_idx, inner_y, inner_x), (n_comps, width_px, width_px)
    )
    fetched = patch_px.astype(jnp.float32)
    entry_patch = fetched[:2]
    leaving = fetched[2:]
    first_re, first_im = product(probe_re, probe_im, entry_patch[0], entry_patch[1])
    spread_re, spread_im = transform(first_re, first_im, ahead)
    second_re, second_im = product(spread_re, spread_im, leaving[0], leaving[1])
    far_re, far_im = transform(second_re, second_im, forward)
    excess = far_re * far_re + far_im * far_im - intens[0]
    back_re, back_im = transform(excess * far_re, excess * far_im, backward)
    exit_re, exit_im = product(spread_re, -spread_im, back_re, back_im)
    mid_re, mid_im = product(leaving[0], -leaving[1], back_re, back_im)
    inner_re, inner_im = transform(mid_re, mid_im, behind)
    entry_re, entry_im = product(probe_re, -probe_im, inner_re, inner_im)
    grad_re, grad_im = product(entry_patch[0], -entry_patch[1], inner_re, inner_im)
    patch_grad = jnp.stack([entry_re, entry_im, exit_re, exit_im]).astype(jnp.bfloat16)

    region_px = tile_span * tile_edge
    shift_y = one_hot(jnp.arange(region_px, dtype=jnp.int32) - inner_y, width_px)
    shift_x = one_hot(jnp.arange(region_px, dtype=jnp.int32) - inner_x, width_px)
    shift_y = shift_y.reshape(tile_span, tile_edge, width_px)
    shift_x = shift_x.reshape(tile_span, tile_edge, width_px)
    rows_cut = jnp.einsum("irk,ckm->cirm", shift_y, patch_grad, preferred_element_type=jnp.float32)
    rows_cut = rows_cut.astype(jnp.bfloat16)
    tiles_cut = jnp.einsum("cirm,jsm->ijcrs", rows_cut, shift_x, preferred_element_type=jnp.float32)
    tiles_cut = tiles_cut.astype(jnp.bfloat16).reshape(
        tile_span * tile_span, n_comps, tile_edge * tile_edge
    )
    outgoing = jnp.dot(
        one_hot(my_owner, owners).T,
        tiles_cut.reshape(tile_span * tile_span, n_comps * tile_edge * tile_edge),
        preferred_element_type=jnp.float32,
    )
    outgoing = outgoing.astype(jnp.bfloat16).reshape(owners, n_comps, tile_edge * tile_edge)
    returned = lax.all_to_all(outgoing, "pos", split_axis=0, concat_axis=0, tiled=True)
    selector = one_hot(send_local, tiles_dev, send_live).T
    local_sum = jnp.dot(
        selector,
        returned.reshape(owners, n_comps * tile_edge * tile_edge),
        preferred_element_type=jnp.float32,
    )
    probe_part = jnp.stack([grad_re, grad_im])
    tile_total = lax.psum(local_sum, "tile")
    probe_total = reduce_probe(probe_part, owners, layers)
    return (tile_total.reshape(tiles_dev, n_comps, tile_edge * tile_edge), probe_total)


def reduce_probe(probe_part, owners, layers):
    piece_len = probe_part.size // owners
    pieces = probe_part.reshape(owners, piece_len)
    mine = jnp.sum(lax.all_to_all(pieces, "pos", 0, 0, tiled=True), axis=0)
    spread = jnp.broadcast_to(mine[None], (layers, piece_len))
    mine = jnp.sum(lax.all_to_all(spread, "tile", 0, 0, tiled=True), axis=0)
    spread = jnp.broadcast_to(mine[None], (owners, piece_len))
    gathered = lax.all_to_all(spread, "pos", 0, 0, tiled=True)
    return gathered.reshape(probe_part.shape)


def solution(mesh):
    in_specs = (P("pos", None, None), P(), P(), P(), P(("pos", "tile"), None, None))
    out_specs = (P("pos", None, None), P())
    return jax.shard_map(
        per_device, mesh=mesh, in_specs=in_specs, out_specs=out_specs, check_vma=False
    )
```

```python
import math

import jax
import jax.numpy as jnp
from jax import lax
from jax.sharding import PartitionSpec as P

TS = 64
OWN_R = 8


def matmul_hi(left_op, right_op):
    return jnp.dot(
        left_op, right_op, precision=lax.Precision.HIGHEST, preferred_element_type=jnp.float32
    )


def spectral_tables(width_px):
    positions = jnp.arange(width_px, dtype=jnp.int32)
    phase_idx = positions[:, None] * positions[None, :] % width_px
    angles = phase_idx.astype(jnp.float32) * (2.0 * math.pi / width_px)
    norm_factor = 1.0 / math.sqrt(width_px)
    return (jnp.cos(angles) * norm_factor, -jnp.sin(angles) * norm_factor)


def complex_matmul(left_re, left_im, right_re, right_im):
    out_re = matmul_hi(left_re, right_re) - matmul_hi(left_im, right_im)
    out_im = matmul_hi(left_re, right_im) + matmul_hi(left_im, right_re)
    return (out_re, out_im)


def propagation_matrix(width_px, fwd_re, fwd_im, sign_val):
    positions = jnp.arange(width_px, dtype=jnp.int32)
    centred = (positions + width_px // 2) % width_px - width_px // 2
    angles = (centred * centred).astype(jnp.float32) * (-0.2 / width_px) * sign_val
    phase_re = jnp.cos(angles)[:, None]
    phase_im = jnp.sin(angles)[:, None]
    scaled_re = phase_re * fwd_re - phase_im * fwd_im
    scaled_im = phase_re * fwd_im + phase_im * fwd_re
    return complex_matmul(fwd_re, -fwd_im, scaled_re, scaled_im)


def stacked_table(table_re, table_im):
    column = jnp.concatenate([table_re, table_im], axis=0)
    block = jnp.concatenate(
        [jnp.concatenate([table_re, -table_im], axis=1), jnp.concatenate([table_im, table_re], axis=1)],
        axis=0,
    )
    return column, block


def transform(part_re, part_im, table):
    column, block = table
    left = jnp.concatenate(
        [jnp.concatenate([part_re, -part_im], axis=1), jnp.concatenate([part_im, part_re], axis=1)],
        axis=0,
    )
    mid = matmul_hi(left, column)
    out = matmul_hi(block, mid)
    width = part_re.shape[0]
    return out[:width], out[width:]


def product(left_re, left_im, right_re, right_im):
    return (left_re * right_re - left_im * right_im, left_re * right_im + left_im * right_re)


def one_hot(index, size, live=None):
    hit = index[:, None] == jnp.arange(size, dtype=index.dtype)[None, :]
    if live is not None:
        hit = hit & live[:, None]
    return hit.astype(jnp.bfloat16)


def per_device(obj_tiles, tile_map, offsets, probe, intens):
    owners = lax.axis_size("pos")
    layers = lax.axis_size("tile")
    me_pos = lax.axis_index("pos")
    me_tile = lax.axis_index("tile")
    tiles_dev = obj_tiles.shape[0]
    n_comps = obj_tiles.shape[1]
    tile_edge = TS
    width_px = probe.shape[-1]
    tile_span = width_px // tile_edge + 1
    own_c = owners // OWN_R
    grid_r, grid_c = tile_map.shape
    span_idx = jnp.arange(tile_span, dtype=jnp.int32)

    mine = (tile_map // tiles_dev) == me_pos
    local_plus = jnp.where(mine, tile_map - me_pos * tiles_dev + 1, 0).astype(jnp.bfloat16)
    by_device = offsets.reshape(owners, layers, 2)
    peer_corners = lax.dynamic_index_in_dim(by_device, me_tile, 1, keepdims=False)
    peer_r = peer_corners[:, 0:1] // tile_edge
    peer_c = peer_corners[:, 1:2] // tile_edge
    grid_rows = jnp.arange(grid_r, dtype=jnp.int32)[None, :]
    grid_cols = jnp.arange(grid_c, dtype=jnp.int32)[None, :]
    row_in = ((grid_rows >= peer_r) & (grid_rows < peer_r + tile_span)).astype(jnp.bfloat16)
    col_in = ((grid_cols >= peer_c) & (grid_cols < peer_c + tile_span)).astype(jnp.float32)
    by_col = jnp.dot(row_in, local_plus, preferred_element_type=jnp.float32)
    found = jnp.sum(by_col * col_in, axis=1).astype(jnp.int32)
    send_live = found > 0
    send_local = jnp.maximum(found - 1, 0)
    chosen = obj_tiles[send_local]

    my_corner = lax.dynamic_index_in_dim(offsets, me_pos * layers + me_tile, 0, keepdims=False)
    row_ids = my_corner[0] // tile_edge + span_idx
    col_ids = my_corner[1] // tile_edge + span_idx
    my_owner = (tile_map[row_ids[:, None], col_ids[None, :]] // tiles_dev).reshape(-1)
    inner_y = my_corner[0] % tile_edge
    inner_x = my_corner[1] % tile_edge
    zero_idx = jnp.zeros((), jnp.int32)
    fwd_re, fwd_im = spectral_tables(width_px)
    ahead_re, ahead_im = propagation_matrix(width_px, fwd_re, fwd_im, 1.0)
    behind_re, behind_im = propagation_matrix(width_px, fwd_re, fwd_im, -1.0)
    ahead = stacked_table(ahead_re, ahead_im)
    forward = stacked_table(fwd_re, fwd_im)
    backward = stacked_table(fwd_re, -fwd_im)
    behind = stacked_table(behind_re, behind_im)
    probe_re = probe[0]
    probe_im = probe[1]
    received = lax.all_to_all(chosen, "pos", split_axis=0, concat_axis=0, tiled=True)
    pieces = received[my_owner]
    region = pieces.reshape(tile_span, tile_span, n_comps, tile_edge, tile_edge).transpose(
        2, 0, 3, 1, 4
    )
    region = region.reshape(n_comps, tile_span * tile_edge, tile_span * tile_edge)
    patch_px = lax.dynamic_slice(
        region, (zero_idx, inner_y, inner_x), (n_comps, width_px, width_px)
    )
    fetched = patch_px.astype(jnp.float32)
    entry_patch = fetched[:2]
    leaving = fetched[2:]
    first_re, first_im = product(probe_re, probe_im, entry_patch[0], entry_patch[1])
    spread_re, spread_im = transform(first_re, first_im, ahead)
    second_re, second_im = product(spread_re, spread_im, leaving[0], leaving[1])
    far_re, far_im = transform(second_re, second_im, forward)
    excess = far_re * far_re + far_im * far_im - intens[0]
    back_re, back_im = transform(excess * far_re, excess * far_im, backward)
    exit_re, exit_im = product(spread_re, -spread_im, back_re, back_im)
    mid_re, mid_im = product(leaving[0], -leaving[1], back_re, back_im)
    inner_re, inner_im = transform(mid_re, mid_im, behind)
    entry_re, entry_im = product(probe_re, -probe_im, inner_re, inner_im)
    grad_re, grad_im = product(entry_patch[0], -entry_patch[1], inner_re, inner_im)
    patch_grad = jnp.stack([entry_re, entry_im, exit_re, exit_im]).astype(jnp.bfloat16)

    region_px = tile_span * tile_edge
    shift_y = one_hot(jnp.arange(region_px, dtype=jnp.int32) - inner_y, width_px)
    shift_x = one_hot(jnp.arange(region_px, dtype=jnp.int32) - inner_x, width_px)
    shift_y = shift_y.reshape(tile_span, tile_edge, width_px)
    shift_x = shift_x.reshape(tile_span, tile_edge, width_px)
    rows_cut = jnp.einsum("irk,ckm->cirm", shift_y, patch_grad, preferred_element_type=jnp.float32)
    rows_cut = rows_cut.astype(jnp.bfloat16)
    tiles_cut = jnp.einsum("cirm,jsm->ijcrs", rows_cut, shift_x, preferred_element_type=jnp.float32)
    n_foot = tile_span * tile_span
    tile_px = n_comps * tile_edge * tile_edge
    tiles_cut = tiles_cut.astype(jnp.bfloat16).reshape(n_foot, tile_px)

    cut_len = -(-tile_px // layers)
    cut_len = -(-cut_len // 128) * 128
    pad_px = cut_len * layers - tile_px
    cut = jnp.pad(tiles_cut, ((0, 0), (0, pad_px))).reshape(n_foot, layers, cut_len)
    from_column = lax.all_to_all(cut.transpose(1, 0, 2), "tile", 0, 0, tiled=True)

    col_corners = lax.dynamic_index_in_dim(by_device, me_pos, 0, keepdims=False)
    col_rows = col_corners[:, 0:1] // tile_edge + span_idx[None, :]
    col_cols = col_corners[:, 1:2] // tile_edge + span_idx[None, :]
    col_owner = tile_map[col_rows[:, :, None], col_cols[:, None, :]].reshape(layers, n_foot)
    col_owner = col_owner // tiles_dev
    to_owner = (col_owner[:, :, None] == jnp.arange(owners)[None, None, :]).astype(jnp.bfloat16)
    outgoing = jnp.einsum("tsp,tsx->ptx", to_owner, from_column, preferred_element_type=jnp.float32)
    outgoing = outgoing.astype(jnp.bfloat16)
    returned = lax.all_to_all(outgoing, "pos", 0, 0, tiled=True)

    all_r = offsets[:, 0:1] // tile_edge
    all_c = offsets[:, 1:2] // tile_edge
    all_row_in = ((grid_rows >= all_r) & (grid_rows < all_r + tile_span)).astype(jnp.bfloat16)
    all_col_in = ((grid_cols >= all_c) & (grid_cols < all_c + tile_span)).astype(jnp.float32)
    all_found = jnp.sum(
        jnp.dot(all_row_in, local_plus, preferred_element_type=jnp.float32) * all_col_in, axis=1
    ).astype(jnp.int32)
    all_sel = one_hot(jnp.maximum(all_found - 1, 0), tiles_dev, all_found > 0)
    all_sel = all_sel.reshape(owners, layers, tiles_dev)
    my_slice = jnp.einsum("qtk,qtx->kx", all_sel, returned, preferred_element_type=jnp.float32)

    probe_part = jnp.stack([grad_re, grad_im])
    piece_len = probe_part.size // owners
    probe_row = jnp.sum(
        lax.all_to_all(probe_part.reshape(owners, piece_len), "pos", 0, 0, tiled=True), axis=0
    )
    probe_cut = jnp.pad(probe_row, (0, cut_len - piece_len))[None]
    gathered = ring_gather(jnp.concatenate([my_slice, probe_cut], axis=0), layers)
    slices = gathered[:, :tiles_dev]
    tile_total = slices.transpose(1, 0, 2).reshape(tiles_dev, layers * cut_len)[:, :tile_px]
    probe_piece = jnp.sum(gathered[:, tiles_dev, :piece_len], axis=0)
    spread = jnp.broadcast_to(probe_piece[None], (owners, piece_len))
    probe_total = lax.all_to_all(spread, "pos", 0, 0, tiled=True).reshape(probe_part.shape)
    return (tile_total.reshape(tiles_dev, n_comps, tile_edge * tile_edge), probe_total)


def ring_gather(values, size):
    me = lax.axis_index("tile")
    to_right = [(i, (i + 1) % size) for i in range(size)]
    to_left = [(i, (i - 1) % size) for i in range(size)]
    back = [values]
    ahead = []
    going_right = values
    going_left = values
    for step in range(1, size // 2 + 1):
        going_right = lax.ppermute(going_right, "tile", to_right)
        back.append(going_right)
        if step < size - size // 2:
            going_left = lax.ppermute(going_left, "tile", to_left)
            ahead.append(going_left)
    by_offset = [back[0]] + ahead + [back[size - d] for d in range(len(ahead) + 1, size)]
    gathered = jnp.zeros((size,) + values.shape, values.dtype)
    for offset, part in enumerate(by_offset):
        gathered = lax.dynamic_update_index_in_dim(gathered, part, (me + offset) % size, 0)
    return gathered


def reduce_probe(probe_part, owners, layers):
    piece_len = probe_part.size // owners
    pieces = probe_part.reshape(owners, piece_len)
    mine = jnp.sum(lax.all_to_all(pieces, "pos", 0, 0, tiled=True), axis=0)
    spread = jnp.broadcast_to(mine[None], (layers, piece_len))
    mine = jnp.sum(lax.all_to_all(spread, "tile", 0, 0, tiled=True), axis=0)
    spread = jnp.broadcast_to(mine[None], (owners, piece_len))
    gathered = lax.all_to_all(spread, "pos", 0, 0, tiled=True)
    return gathered.reshape(probe_part.shape)


def solution(mesh):
    in_specs = (P("pos", None, None), P(), P(), P(), P(("pos", "tile"), None, None))
    out_specs = (P("pos", None, None), P())
    return jax.shard_map(
        per_device, mesh=mesh, in_specs=in_specs, out_specs=out_specs, check_vma=False
    )
```

```python
import math

import jax
import jax.numpy as jnp
from jax import lax
from jax.sharding import PartitionSpec as P

TS = 64
OWN_R = 8


def matmul_hi(left_op, right_op):
    return jnp.dot(
        left_op, right_op, precision=lax.Precision.HIGHEST, preferred_element_type=jnp.float32
    )


def spectral_tables(width_px):
    positions = jnp.arange(width_px, dtype=jnp.int32)
    phase_idx = positions[:, None] * positions[None, :] % width_px
    angles = phase_idx.astype(jnp.float32) * (2.0 * math.pi / width_px)
    norm_factor = 1.0 / math.sqrt(width_px)
    return (jnp.cos(angles) * norm_factor, -jnp.sin(angles) * norm_factor)


def complex_matmul(left_re, left_im, right_re, right_im):
    out_re = matmul_hi(left_re, right_re) - matmul_hi(left_im, right_im)
    out_im = matmul_hi(left_re, right_im) + matmul_hi(left_im, right_re)
    return (out_re, out_im)


def propagation_matrix(width_px, fwd_re, fwd_im, sign_val):
    positions = jnp.arange(width_px, dtype=jnp.int32)
    centred = (positions + width_px // 2) % width_px - width_px // 2
    angles = (centred * centred).astype(jnp.float32) * (-0.2 / width_px) * sign_val
    phase_re = jnp.cos(angles)[:, None]
    phase_im = jnp.sin(angles)[:, None]
    scaled_re = phase_re * fwd_re - phase_im * fwd_im
    scaled_im = phase_re * fwd_im + phase_im * fwd_re
    return complex_matmul(fwd_re, -fwd_im, scaled_re, scaled_im)


def stacked_table(table_re, table_im):
    column = jnp.concatenate([table_re, table_im], axis=0)
    block = jnp.concatenate(
        [jnp.concatenate([table_re, -table_im], axis=1), jnp.concatenate([table_im, table_re], axis=1)],
        axis=0,
    )
    return column, block


def transform(part_re, part_im, table):
    column, block = table
    left = jnp.concatenate(
        [jnp.concatenate([part_re, -part_im], axis=1), jnp.concatenate([part_im, part_re], axis=1)],
        axis=0,
    )
    mid = matmul_hi(left, column)
    out = matmul_hi(block, mid)
    width = part_re.shape[0]
    return out[:width], out[width:]


def product(left_re, left_im, right_re, right_im):
    return (left_re * right_re - left_im * right_im, left_re * right_im + left_im * right_re)


def one_hot(index, size, live=None):
    hit = index[:, None] == jnp.arange(size, dtype=index.dtype)[None, :]
    if live is not None:
        hit = hit & live[:, None]
    return hit.astype(jnp.bfloat16)


def per_device(obj_tiles, tile_map, offsets, probe, intens):
    owners = lax.axis_size("pos")
    layers = lax.axis_size("tile")
    me_pos = lax.axis_index("pos")
    me_tile = lax.axis_index("tile")
    tiles_dev = obj_tiles.shape[0]
    n_comps = obj_tiles.shape[1]
    tile_edge = TS
    width_px = probe.shape[-1]
    tile_span = width_px // tile_edge + 1
    own_c = owners // OWN_R
    grid_r, grid_c = tile_map.shape
    span_idx = jnp.arange(tile_span, dtype=jnp.int32)

    mine = (tile_map // tiles_dev) == me_pos
    local_plus = jnp.where(mine, tile_map - me_pos * tiles_dev + 1, 0).astype(jnp.bfloat16)
    by_device = offsets.reshape(owners, layers, 2)
    peer_corners = lax.dynamic_index_in_dim(by_device, me_tile, 1, keepdims=False)
    peer_r = peer_corners[:, 0:1] // tile_edge
    peer_c = peer_corners[:, 1:2] // tile_edge
    grid_rows = jnp.arange(grid_r, dtype=jnp.int32)[None, :]
    grid_cols = jnp.arange(grid_c, dtype=jnp.int32)[None, :]
    row_in = ((grid_rows >= peer_r) & (grid_rows < peer_r + tile_span)).astype(jnp.bfloat16)
    col_in = ((grid_cols >= peer_c) & (grid_cols < peer_c + tile_span)).astype(jnp.float32)
    by_col = jnp.dot(row_in, local_plus, preferred_element_type=jnp.float32)
    found = jnp.sum(by_col * col_in, axis=1).astype(jnp.int32)
    send_live = found > 0
    send_local = jnp.maximum(found - 1, 0)
    chosen = obj_tiles[send_local]

    my_corner = lax.dynamic_index_in_dim(offsets, me_pos * layers + me_tile, 0, keepdims=False)
    row_ids = my_corner[0] // tile_edge + span_idx
    col_ids = my_corner[1] // tile_edge + span_idx
    my_owner = (tile_map[row_ids[:, None], col_ids[None, :]] // tiles_dev).reshape(-1)
    inner_y = my_corner[0] % tile_edge
    inner_x = my_corner[1] % tile_edge
    zero_idx = jnp.zeros((), jnp.int32)
    fwd_re, fwd_im = spectral_tables(width_px)
    ahead_re, ahead_im = propagation_matrix(width_px, fwd_re, fwd_im, 1.0)
    behind_re, behind_im = propagation_matrix(width_px, fwd_re, fwd_im, -1.0)
    ahead = stacked_table(ahead_re, ahead_im)
    forward = stacked_table(fwd_re, fwd_im)
    backward = stacked_table(fwd_re, -fwd_im)
    behind = stacked_table(behind_re, behind_im)
    probe_re = probe[0]
    probe_im = probe[1]
    received = lax.all_to_all(chosen, "pos", split_axis=0, concat_axis=0, tiled=True)
    pieces = received[my_owner]
    region = pieces.reshape(tile_span, tile_span, n_comps, tile_edge, tile_edge).transpose(
        2, 0, 3, 1, 4
    )
    region = region.reshape(n_comps, tile_span * tile_edge, tile_span * tile_edge)
    patch_px = lax.dynamic_slice(
        region, (zero_idx, inner_y, inner_x), (n_comps, width_px, width_px)
    )
    fetched = patch_px.astype(jnp.float32)
    entry_patch = fetched[:2]
    leaving = fetched[2:]
    first_re, first_im = product(probe_re, probe_im, entry_patch[0], entry_patch[1])
    spread_re, spread_im = transform(first_re, first_im, ahead)
    second_re, second_im = product(spread_re, spread_im, leaving[0], leaving[1])
    far_re, far_im = transform(second_re, second_im, forward)
    excess = far_re * far_re + far_im * far_im - intens[0]
    back_re, back_im = transform(excess * far_re, excess * far_im, backward)
    exit_re, exit_im = product(spread_re, -spread_im, back_re, back_im)
    mid_re, mid_im = product(leaving[0], -leaving[1], back_re, back_im)
    inner_re, inner_im = transform(mid_re, mid_im, behind)
    entry_re, entry_im = product(probe_re, -probe_im, inner_re, inner_im)
    grad_re, grad_im = product(entry_patch[0], -entry_patch[1], inner_re, inner_im)
    patch_grad = jnp.stack([entry_re, entry_im, exit_re, exit_im]).astype(jnp.bfloat16)

    region_px = tile_span * tile_edge
    shift_y = one_hot(jnp.arange(region_px, dtype=jnp.int32) - inner_y, width_px)
    shift_x = one_hot(jnp.arange(region_px, dtype=jnp.int32) - inner_x, width_px)
    shift_y = shift_y.reshape(tile_span, tile_edge, width_px)
    shift_x = shift_x.reshape(tile_span, tile_edge, width_px)
    rows_cut = jnp.einsum("irk,ckm->cirm", shift_y, patch_grad, preferred_element_type=jnp.float32)
    rows_cut = rows_cut.astype(jnp.bfloat16)
    tiles_cut = jnp.einsum("cirm,jsm->ijcrs", rows_cut, shift_x, preferred_element_type=jnp.float32)
    n_foot = tile_span * tile_span
    tile_px = n_comps * tile_edge * tile_edge
    tiles_cut = tiles_cut.astype(jnp.bfloat16).reshape(n_foot, tile_px)

    cut_len = -(-tile_px // layers)
    cut_len = -(-cut_len // 128) * 128
    pad_px = cut_len * layers - tile_px
    cut = jnp.pad(tiles_cut, ((0, 0), (0, pad_px))).reshape(n_foot, layers, cut_len)
    cut = cut.transpose(1, 0, 2).reshape(layers, n_foot, cut_len // 128, 128)
    from_column = lax.all_to_all(cut, "tile", 0, 0, tiled=True)
    from_column = from_column.reshape(layers, n_foot, cut_len)

    col_corners = lax.dynamic_index_in_dim(by_device, me_pos, 0, keepdims=False)
    col_rows = col_corners[:, 0:1] // tile_edge + span_idx[None, :]
    col_cols = col_corners[:, 1:2] // tile_edge + span_idx[None, :]
    col_owner = tile_map[col_rows[:, :, None], col_cols[:, None, :]].reshape(layers, n_foot)
    col_owner = col_owner // tiles_dev
    to_owner = (col_owner[:, :, None] == jnp.arange(owners)[None, None, :]).astype(jnp.bfloat16)
    by_owner = jnp.einsum("tsp,tsx->ptx", to_owner, from_column, preferred_element_type=jnp.float32)
    by_owner = by_owner.astype(jnp.bfloat16).reshape(owners, layers * cut_len)

    probe_part = jnp.stack([grad_re, grad_im])
    piece_len = probe_part.size // owners
    probe_hi = probe_part.reshape(owners, piece_len).astype(jnp.bfloat16)
    probe_lo = (probe_part.reshape(owners, piece_len) - probe_hi.astype(jnp.float32)).astype(jnp.bfloat16)
    slot_len = layers * cut_len + 2 * piece_len
    slot_len = -(-slot_len // 128) * 128
    outgoing = jnp.concatenate([by_owner, probe_hi, probe_lo], axis=1)
    outgoing = jnp.pad(outgoing, ((0, 0), (0, slot_len - outgoing.shape[1])))
    outgoing = outgoing.reshape(owners, slot_len // 128, 128)
    returned = lax.all_to_all(outgoing, "pos", 0, 0, tiled=True).reshape(owners, slot_len)
    from_owners = returned[:, : layers * cut_len].reshape(owners, layers, cut_len)
    probe_back = returned[:, layers * cut_len : layers * cut_len + 2 * piece_len].astype(jnp.float32)
    probe_row = jnp.sum(probe_back[:, :piece_len], axis=0) + jnp.sum(probe_back[:, piece_len:], axis=0)

    all_r = offsets[:, 0:1] // tile_edge
    all_c = offsets[:, 1:2] // tile_edge
    all_row_in = ((grid_rows >= all_r) & (grid_rows < all_r + tile_span)).astype(jnp.bfloat16)
    all_col_in = ((grid_cols >= all_c) & (grid_cols < all_c + tile_span)).astype(jnp.float32)
    all_found = jnp.sum(
        jnp.dot(all_row_in, local_plus, preferred_element_type=jnp.float32) * all_col_in, axis=1
    ).astype(jnp.int32)
    all_sel = one_hot(jnp.maximum(all_found - 1, 0), tiles_dev, all_found > 0)
    all_sel = all_sel.reshape(owners, layers, tiles_dev)
    my_slice = jnp.einsum("qtk,qtx->kx", all_sel, from_owners, preferred_element_type=jnp.float32)

    probe_cut = jnp.pad(probe_row, (0, cut_len - piece_len))[None]
    gathered = ring_gather(jnp.concatenate([my_slice, probe_cut], axis=0), layers)
    slices = gathered[:, :tiles_dev]
    tile_total = slices.transpose(1, 0, 2).reshape(tiles_dev, layers * cut_len)[:, :tile_px]
    probe_piece = jnp.sum(gathered[:, tiles_dev, :piece_len], axis=0)
    spread = jnp.broadcast_to(probe_piece[None], (owners, piece_len))
    probe_total = lax.all_to_all(spread, "pos", 0, 0, tiled=True).reshape(probe_part.shape)
    return (tile_total.reshape(tiles_dev, n_comps, tile_edge * tile_edge), probe_total)


def ring_gather(values, size):
    me = lax.axis_index("tile")
    to_right = [(i, (i + 1) % size) for i in range(size)]
    to_left = [(i, (i - 1) % size) for i in range(size)]
    back = [values]
    ahead = []
    going_right = values
    going_left = values
    for step in range(1, size // 2 + 1):
        going_right = lax.ppermute(going_right, "tile", to_right)
        back.append(going_right)
        if step < size - size // 2:
            going_left = lax.ppermute(going_left, "tile", to_left)
            ahead.append(going_left)
    by_offset = [back[0]] + ahead + [back[size - d] for d in range(len(ahead) + 1, size)]
    order = (jnp.arange(size, dtype=jnp.int32) - me) % size
    return jnp.stack(by_offset)[order]


def reduce_probe(probe_part, owners, layers):
    piece_len = probe_part.size // owners
    pieces = probe_part.reshape(owners, piece_len)
    mine = jnp.sum(lax.all_to_all(pieces, "pos", 0, 0, tiled=True), axis=0)
    spread = jnp.broadcast_to(mine[None], (layers, piece_len))
    mine = jnp.sum(lax.all_to_all(spread, "tile", 0, 0, tiled=True), axis=0)
    spread = jnp.broadcast_to(mine[None], (owners, piece_len))
    gathered = lax.all_to_all(spread, "pos", 0, 0, tiled=True)
    return gathered.reshape(probe_part.shape)


def solution(mesh):
    in_specs = (P("pos", None, None), P(), P(), P(), P(("pos", "tile"), None, None))
    out_specs = (P("pos", None, None), P())
    return jax.shard_map(
        per_device, mesh=mesh, in_specs=in_specs, out_specs=out_specs, check_vma=False
    )
```

```python
import math

import jax
import jax.numpy as jnp
from jax import lax
from jax.sharding import PartitionSpec as P

TS = 64
OWN_R = 8


def matmul_hi(left_op, right_op):
    return jnp.dot(
        left_op, right_op, precision=lax.Precision.HIGHEST, preferred_element_type=jnp.float32
    )


def spectral_tables(width_px):
    positions = jnp.arange(width_px, dtype=jnp.int32)
    phase_idx = positions[:, None] * positions[None, :] % width_px
    angles = phase_idx.astype(jnp.float32) * (2.0 * math.pi / width_px)
    norm_factor = 1.0 / math.sqrt(width_px)
    return (jnp.cos(angles) * norm_factor, -jnp.sin(angles) * norm_factor)


def complex_matmul(left_re, left_im, right_re, right_im):
    out_re = matmul_hi(left_re, right_re) - matmul_hi(left_im, right_im)
    out_im = matmul_hi(left_re, right_im) + matmul_hi(left_im, right_re)
    return (out_re, out_im)


def propagation_matrix(width_px, fwd_re, fwd_im, sign_val):
    positions = jnp.arange(width_px, dtype=jnp.int32)
    centred = (positions + width_px // 2) % width_px - width_px // 2
    angles = (centred * centred).astype(jnp.float32) * (-0.2 / width_px) * sign_val
    phase_re = jnp.cos(angles)[:, None]
    phase_im = jnp.sin(angles)[:, None]
    scaled_re = phase_re * fwd_re - phase_im * fwd_im
    scaled_im = phase_re * fwd_im + phase_im * fwd_re
    return complex_matmul(fwd_re, -fwd_im, scaled_re, scaled_im)


def stacked_table(table_re, table_im):
    column = jnp.concatenate([table_re, table_im], axis=0)
    block = jnp.concatenate(
        [jnp.concatenate([table_re, -table_im], axis=1), jnp.concatenate([table_im, table_re], axis=1)],
        axis=0,
    )
    return column, block


def transform(part_re, part_im, table):
    column, block = table
    left = jnp.concatenate(
        [jnp.concatenate([part_re, -part_im], axis=1), jnp.concatenate([part_im, part_re], axis=1)],
        axis=0,
    )
    mid = matmul_hi(left, column)
    out = matmul_hi(block, mid)
    width = part_re.shape[0]
    return out[:width], out[width:]


def product(left_re, left_im, right_re, right_im):
    return (left_re * right_re - left_im * right_im, left_re * right_im + left_im * right_re)


def one_hot(index, size, live=None):
    hit = index[:, None] == jnp.arange(size, dtype=index.dtype)[None, :]
    if live is not None:
        hit = hit & live[:, None]
    return hit.astype(jnp.bfloat16)


def per_device(obj_tiles, tile_map, offsets, probe, intens):
    owners = lax.axis_size("pos")
    layers = lax.axis_size("tile")
    me_pos = lax.axis_index("pos")
    me_tile = lax.axis_index("tile")
    tiles_dev = obj_tiles.shape[0]
    n_comps = obj_tiles.shape[1]
    tile_edge = TS
    width_px = probe.shape[-1]
    tile_span = width_px // tile_edge + 1
    own_c = owners // OWN_R
    grid_r, grid_c = tile_map.shape
    span_idx = jnp.arange(tile_span, dtype=jnp.int32)

    mine = (tile_map // tiles_dev) == me_pos
    local_plus = jnp.where(mine, tile_map - me_pos * tiles_dev + 1, 0).astype(jnp.bfloat16)
    by_device = offsets.reshape(owners, layers, 2)
    peer_corners = lax.dynamic_index_in_dim(by_device, me_tile, 1, keepdims=False)
    peer_r = peer_corners[:, 0:1] // tile_edge
    peer_c = peer_corners[:, 1:2] // tile_edge
    grid_rows = jnp.arange(grid_r, dtype=jnp.int32)[None, :]
    grid_cols = jnp.arange(grid_c, dtype=jnp.int32)[None, :]
    row_in = ((grid_rows >= peer_r) & (grid_rows < peer_r + tile_span)).astype(jnp.bfloat16)
    col_in = ((grid_cols >= peer_c) & (grid_cols < peer_c + tile_span)).astype(jnp.float32)
    by_col = jnp.dot(row_in, local_plus, preferred_element_type=jnp.float32)
    found = jnp.sum(by_col * col_in, axis=1).astype(jnp.int32)
    send_live = found > 0
    send_local = jnp.maximum(found - 1, 0)
    chosen = obj_tiles[send_local]

    my_corner = lax.dynamic_index_in_dim(offsets, me_pos * layers + me_tile, 0, keepdims=False)
    row_ids = my_corner[0] // tile_edge + span_idx
    col_ids = my_corner[1] // tile_edge + span_idx
    my_owner = (tile_map[row_ids[:, None], col_ids[None, :]] // tiles_dev).reshape(-1)
    inner_y = my_corner[0] % tile_edge
    inner_x = my_corner[1] % tile_edge
    zero_idx = jnp.zeros((), jnp.int32)
    fwd_re, fwd_im = spectral_tables(width_px)
    ahead_re, ahead_im = propagation_matrix(width_px, fwd_re, fwd_im, 1.0)
    behind_re, behind_im = propagation_matrix(width_px, fwd_re, fwd_im, -1.0)
    ahead = stacked_table(ahead_re, ahead_im)
    forward = stacked_table(fwd_re, fwd_im)
    backward = stacked_table(fwd_re, -fwd_im)
    behind = stacked_table(behind_re, behind_im)
    probe_re = probe[0]
    probe_im = probe[1]
    received = lax.all_to_all(chosen, "pos", split_axis=0, concat_axis=0, tiled=True)
    pieces = received[my_owner]
    region = pieces.reshape(tile_span, tile_span, n_comps, tile_edge, tile_edge).transpose(
        2, 0, 3, 1, 4
    )
    region = region.reshape(n_comps, tile_span * tile_edge, tile_span * tile_edge)
    patch_px = lax.dynamic_slice(
        region, (zero_idx, inner_y, inner_x), (n_comps, width_px, width_px)
    )
    fetched = patch_px.astype(jnp.float32)
    entry_patch = fetched[:2]
    leaving = fetched[2:]
    first_re, first_im = product(probe_re, probe_im, entry_patch[0], entry_patch[1])
    spread_re, spread_im = transform(first_re, first_im, ahead)
    second_re, second_im = product(spread_re, spread_im, leaving[0], leaving[1])
    far_re, far_im = transform(second_re, second_im, forward)
    excess = far_re * far_re + far_im * far_im - intens[0]
    back_re, back_im = transform(excess * far_re, excess * far_im, backward)
    exit_re, exit_im = product(spread_re, -spread_im, back_re, back_im)
    mid_re, mid_im = product(leaving[0], -leaving[1], back_re, back_im)
    inner_re, inner_im = transform(mid_re, mid_im, behind)
    entry_re, entry_im = product(probe_re, -probe_im, inner_re, inner_im)
    grad_re, grad_im = product(entry_patch[0], -entry_patch[1], inner_re, inner_im)
    patch_grad = jnp.stack([entry_re, entry_im, exit_re, exit_im]).astype(jnp.bfloat16)

    region_px = tile_span * tile_edge
    shift_y = one_hot(jnp.arange(region_px, dtype=jnp.int32) - inner_y, width_px)
    shift_x = one_hot(jnp.arange(region_px, dtype=jnp.int32) - inner_x, width_px)
    shift_y = shift_y.reshape(tile_span, tile_edge, width_px)
    shift_x = shift_x.reshape(tile_span, tile_edge, width_px)
    rows_cut = jnp.einsum("irk,ckm->cirm", shift_y, patch_grad, preferred_element_type=jnp.float32)
    rows_cut = rows_cut.astype(jnp.bfloat16)
    tiles_cut = jnp.einsum("cirm,jsm->ijcrs", rows_cut, shift_x, preferred_element_type=jnp.float32)
    n_foot = tile_span * tile_span
    tile_px = n_comps * tile_edge * tile_edge
    tiles_cut = tiles_cut.astype(jnp.bfloat16).reshape(n_foot, tile_px)

    cut_len = -(-tile_px // layers)
    cut_len = -(-cut_len // 128) * 128
    pad_px = cut_len * layers - tile_px
    cut = jnp.pad(tiles_cut, ((0, 0), (0, pad_px))).reshape(n_foot, layers, cut_len)
    cut = cut.transpose(1, 0, 2).reshape(layers, n_foot, cut_len // 128, 128)
    from_column = lax.all_to_all(cut, "tile", 0, 0, tiled=True)
    from_column = from_column.reshape(layers, n_foot, cut_len)

    col_corners = lax.dynamic_index_in_dim(by_device, me_pos, 0, keepdims=False)
    col_rows = col_corners[:, 0:1] // tile_edge + span_idx[None, :]
    col_cols = col_corners[:, 1:2] // tile_edge + span_idx[None, :]
    col_owner = tile_map[col_rows[:, :, None], col_cols[:, None, :]].reshape(layers, n_foot)
    col_owner = col_owner // tiles_dev
    to_owner = (col_owner[:, :, None] == jnp.arange(owners)[None, None, :]).astype(jnp.bfloat16)
    by_owner = jnp.einsum("tsp,tsx->ptx", to_owner, from_column, preferred_element_type=jnp.float32)
    by_owner = by_owner.astype(jnp.bfloat16).reshape(owners, layers * cut_len)

    probe_part = jnp.stack([grad_re, grad_im])
    piece_len = probe_part.size // owners
    probe_hi = probe_part.reshape(owners, piece_len).astype(jnp.bfloat16)
    probe_lo = (probe_part.reshape(owners, piece_len) - probe_hi.astype(jnp.float32)).astype(jnp.bfloat16)
    slot_len = layers * cut_len + 2 * piece_len
    slot_len = -(-slot_len // 128) * 128
    outgoing = jnp.concatenate([by_owner, probe_hi, probe_lo], axis=1)
    outgoing = jnp.pad(outgoing, ((0, 0), (0, slot_len - outgoing.shape[1])))
    outgoing = outgoing.reshape(owners, slot_len // 128, 128)
    returned = lax.all_to_all(outgoing, "pos", 0, 0, tiled=True).reshape(owners, slot_len)
    from_owners = returned[:, : layers * cut_len].reshape(owners, layers, cut_len)
    probe_back = returned[:, layers * cut_len : layers * cut_len + 2 * piece_len].astype(jnp.float32)
    probe_row = jnp.sum(probe_back[:, :piece_len], axis=0) + jnp.sum(probe_back[:, piece_len:], axis=0)

    all_r = offsets[:, 0:1] // tile_edge
    all_c = offsets[:, 1:2] // tile_edge
    all_row_in = ((grid_rows >= all_r) & (grid_rows < all_r + tile_span)).astype(jnp.bfloat16)
    all_col_in = ((grid_cols >= all_c) & (grid_cols < all_c + tile_span)).astype(jnp.float32)
    all_found = jnp.sum(
        jnp.dot(all_row_in, local_plus, preferred_element_type=jnp.float32) * all_col_in, axis=1
    ).astype(jnp.int32)
    all_sel = one_hot(jnp.maximum(all_found - 1, 0), tiles_dev, all_found > 0)
    all_sel = all_sel.reshape(owners, layers, tiles_dev)
    my_slice = jnp.einsum("qtk,qtx->kx", all_sel, from_owners, preferred_element_type=jnp.float32)

    spread = jnp.broadcast_to(probe_row[None], (layers, piece_len))
    probe_piece = jnp.sum(lax.all_to_all(spread, "tile", 0, 0, tiled=True), axis=0)
    spread = jnp.broadcast_to(probe_piece[None], (owners, piece_len))
    probe_total = lax.all_to_all(spread, "pos", 0, 0, tiled=True).reshape(probe_part.shape)
    slices = ring_gather(my_slice, layers)
    tile_total = slices.transpose(1, 0, 2).reshape(tiles_dev, layers * cut_len)[:, :tile_px]
    return (tile_total.reshape(tiles_dev, n_comps, tile_edge * tile_edge), probe_total)


def ring_gather(values, size, stride=3):
    me = lax.axis_index("tile")
    if size % stride or size <= stride:
        stride = 1
    groups = size // stride

    def shifted(x, shift):
        return lax.ppermute(x, "tile", [(i, (i + shift) % size) for i in range(size)])

    bundle = jnp.stack([values] + [shifted(values, stride * w) for w in range(1, groups)])
    bundles = [bundle]
    source = {(-stride * w) % size: (0, w) for w in range(groups)}
    for r in range(1, stride):
        shift = r if r <= stride // 2 else r - stride
        bundles.append(shifted(bundle, shift))
        for w in range(groups):
            source[(-shift - stride * w) % size] = (r, w)
    by_offset = jnp.stack([bundles[source[d][0]][source[d][1]] for d in range(size)])
    order = (jnp.arange(size, dtype=jnp.int32) - me) % size
    return by_offset[order]


def reduce_probe(probe_part, owners, layers):
    piece_len = probe_part.size // owners
    pieces = probe_part.reshape(owners, piece_len)
    mine = jnp.sum(lax.all_to_all(pieces, "pos", 0, 0, tiled=True), axis=0)
    spread = jnp.broadcast_to(mine[None], (layers, piece_len))
    mine = jnp.sum(lax.all_to_all(spread, "tile", 0, 0, tiled=True), axis=0)
    spread = jnp.broadcast_to(mine[None], (owners, piece_len))
    gathered = lax.all_to_all(spread, "pos", 0, 0, tiled=True)
    return gathered.reshape(probe_part.shape)


def solution(mesh):
    in_specs = (P("pos", None, None), P(), P(), P(), P(("pos", "tile"), None, None))
    out_specs = (P("pos", None, None), P())
    return jax.shard_map(
        per_device, mesh=mesh, in_specs=in_specs, out_specs=out_specs, check_vma=False
    )
```

```python
import math

import jax
import jax.numpy as jnp
from jax import lax
from jax.sharding import PartitionSpec as P

TS = 64
OWN_R = 8


def matmul_hi(left_op, right_op):
    return jnp.dot(
        left_op, right_op, precision=lax.Precision.HIGHEST, preferred_element_type=jnp.float32
    )


def spectral_tables(width_px):
    positions = jnp.arange(width_px, dtype=jnp.int32)
    phase_idx = positions[:, None] * positions[None, :] % width_px
    angles = phase_idx.astype(jnp.float32) * (2.0 * math.pi / width_px)
    norm_factor = 1.0 / math.sqrt(width_px)
    return (jnp.cos(angles) * norm_factor, -jnp.sin(angles) * norm_factor)


def complex_matmul(left_re, left_im, right_re, right_im):
    out_re = matmul_hi(left_re, right_re) - matmul_hi(left_im, right_im)
    out_im = matmul_hi(left_re, right_im) + matmul_hi(left_im, right_re)
    return (out_re, out_im)


def propagation_matrix(width_px, fwd_re, fwd_im, sign_val):
    positions = jnp.arange(width_px, dtype=jnp.int32)
    centred = (positions + width_px // 2) % width_px - width_px // 2
    angles = (centred * centred).astype(jnp.float32) * (-0.2 / width_px) * sign_val
    phase_re = jnp.cos(angles)[:, None]
    phase_im = jnp.sin(angles)[:, None]
    scaled_re = phase_re * fwd_re - phase_im * fwd_im
    scaled_im = phase_re * fwd_im + phase_im * fwd_re
    return complex_matmul(fwd_re, -fwd_im, scaled_re, scaled_im)


def stacked_table(table_re, table_im):
    column = jnp.concatenate([table_re, table_im], axis=0)
    block = jnp.concatenate(
        [jnp.concatenate([table_re, -table_im], axis=1), jnp.concatenate([table_im, table_re], axis=1)],
        axis=0,
    )
    return column, block


def transform(part_re, part_im, table):
    column, block = table
    left = jnp.concatenate(
        [jnp.concatenate([part_re, -part_im], axis=1), jnp.concatenate([part_im, part_re], axis=1)],
        axis=0,
    )
    mid = matmul_hi(left, column)
    out = matmul_hi(block, mid)
    width = part_re.shape[0]
    return out[:width], out[width:]


def product(left_re, left_im, right_re, right_im):
    return (left_re * right_re - left_im * right_im, left_re * right_im + left_im * right_re)


def one_hot(index, size, live=None):
    hit = index[:, None] == jnp.arange(size, dtype=index.dtype)[None, :]
    if live is not None:
        hit = hit & live[:, None]
    return hit.astype(jnp.bfloat16)


def per_device(obj_tiles, tile_map, offsets, probe, intens):
    owners = lax.axis_size("pos")
    layers = lax.axis_size("tile")
    me_pos = lax.axis_index("pos")
    me_tile = lax.axis_index("tile")
    tiles_dev = obj_tiles.shape[0]
    n_comps = obj_tiles.shape[1]
    tile_edge = TS
    width_px = probe.shape[-1]
    tile_span = width_px // tile_edge + 1
    own_c = owners // OWN_R
    grid_r, grid_c = tile_map.shape
    span_idx = jnp.arange(tile_span, dtype=jnp.int32)

    mine = (tile_map // tiles_dev) == me_pos
    local_plus = jnp.where(mine, tile_map - me_pos * tiles_dev + 1, 0).astype(jnp.bfloat16)
    by_device = offsets.reshape(owners, layers, 2)
    peer_corners = lax.dynamic_index_in_dim(by_device, me_tile, 1, keepdims=False)
    peer_r = peer_corners[:, 0:1] // tile_edge
    peer_c = peer_corners[:, 1:2] // tile_edge
    grid_rows = jnp.arange(grid_r, dtype=jnp.int32)[None, :]
    grid_cols = jnp.arange(grid_c, dtype=jnp.int32)[None, :]
    row_in = ((grid_rows >= peer_r) & (grid_rows < peer_r + tile_span)).astype(jnp.bfloat16)
    col_in = ((grid_cols >= peer_c) & (grid_cols < peer_c + tile_span)).astype(jnp.float32)
    by_col = jnp.dot(row_in, local_plus, preferred_element_type=jnp.float32)
    found = jnp.sum(by_col * col_in, axis=1).astype(jnp.int32)
    send_live = found > 0
    send_local = jnp.maximum(found - 1, 0)
    chosen = obj_tiles[send_local]

    my_corner = lax.dynamic_index_in_dim(offsets, me_pos * layers + me_tile, 0, keepdims=False)
    row_ids = my_corner[0] // tile_edge + span_idx
    col_ids = my_corner[1] // tile_edge + span_idx
    my_owner = (tile_map[row_ids[:, None], col_ids[None, :]] // tiles_dev).reshape(-1)
    inner_y = my_corner[0] % tile_edge
    inner_x = my_corner[1] % tile_edge
    zero_idx = jnp.zeros((), jnp.int32)
    fwd_re, fwd_im = spectral_tables(width_px)
    ahead_re, ahead_im = propagation_matrix(width_px, fwd_re, fwd_im, 1.0)
    behind_re, behind_im = propagation_matrix(width_px, fwd_re, fwd_im, -1.0)
    ahead = stacked_table(ahead_re, ahead_im)
    forward = stacked_table(fwd_re, fwd_im)
    backward = stacked_table(fwd_re, -fwd_im)
    behind = stacked_table(behind_re, behind_im)
    probe_re = probe[0]
    probe_im = probe[1]
    received = lax.all_to_all(chosen, "pos", split_axis=0, concat_axis=0, tiled=True)
    pieces = received[my_owner]
    region = pieces.reshape(tile_span, tile_span, n_comps, tile_edge, tile_edge).transpose(
        2, 0, 3, 1, 4
    )
    region = region.reshape(n_comps, tile_span * tile_edge, tile_span * tile_edge)
    patch_px = lax.dynamic_slice(
        region, (zero_idx, inner_y, inner_x), (n_comps, width_px, width_px)
    )
    fetched = patch_px.astype(jnp.float32)
    entry_patch = fetched[:2]
    leaving = fetched[2:]
    first_re, first_im = product(probe_re, probe_im, entry_patch[0], entry_patch[1])
    spread_re, spread_im = transform(first_re, first_im, ahead)
    second_re, second_im = product(spread_re, spread_im, leaving[0], leaving[1])
    far_re, far_im = transform(second_re, second_im, forward)
    excess = far_re * far_re + far_im * far_im - intens[0]
    back_re, back_im = transform(excess * far_re, excess * far_im, backward)
    exit_re, exit_im = product(spread_re, -spread_im, back_re, back_im)
    mid_re, mid_im = product(leaving[0], -leaving[1], back_re, back_im)
    inner_re, inner_im = transform(mid_re, mid_im, behind)
    entry_re, entry_im = product(probe_re, -probe_im, inner_re, inner_im)
    grad_re, grad_im = product(entry_patch[0], -entry_patch[1], inner_re, inner_im)
    patch_grad = jnp.stack([entry_re, entry_im, exit_re, exit_im]).astype(jnp.bfloat16)

    region_px = tile_span * tile_edge
    shift_y = one_hot(jnp.arange(region_px, dtype=jnp.int32) - inner_y, width_px)
    shift_x = one_hot(jnp.arange(region_px, dtype=jnp.int32) - inner_x, width_px)
    shift_y = shift_y.reshape(tile_span, tile_edge, width_px)
    shift_x = shift_x.reshape(tile_span, tile_edge, width_px)
    rows_cut = jnp.einsum("irk,ckm->cirm", shift_y, patch_grad, preferred_element_type=jnp.float32)
    rows_cut = rows_cut.astype(jnp.bfloat16)
    tiles_cut = jnp.einsum("cirm,jsm->ijcrs", rows_cut, shift_x, preferred_element_type=jnp.float32)
    n_foot = tile_span * tile_span
    tile_px = n_comps * tile_edge * tile_edge
    tiles_cut = tiles_cut.astype(jnp.bfloat16).reshape(n_foot, tile_px)

    cut_len = -(-tile_px // layers)
    cut_len = -(-cut_len // 128) * 128
    pad_px = cut_len * layers - tile_px
    cut = jnp.pad(tiles_cut, ((0, 0), (0, pad_px))).reshape(n_foot, layers, cut_len)
    cut = cut.transpose(1, 0, 2).reshape(layers, n_foot, cut_len // 128, 128)
    from_column = lax.all_to_all(cut, "tile", 0, 0, tiled=True)
    from_column = from_column.reshape(layers, n_foot, cut_len)

    col_corners = lax.dynamic_index_in_dim(by_device, me_pos, 0, keepdims=False)
    col_rows = col_corners[:, 0:1] // tile_edge + span_idx[None, :]
    col_cols = col_corners[:, 1:2] // tile_edge + span_idx[None, :]
    col_owner = tile_map[col_rows[:, :, None], col_cols[:, None, :]].reshape(layers, n_foot)
    col_owner = col_owner // tiles_dev
    to_owner = (col_owner[:, :, None] == jnp.arange(owners)[None, None, :]).astype(jnp.bfloat16)
    by_owner = jnp.einsum("tsp,tsx->ptx", to_owner, from_column, preferred_element_type=jnp.float32)
    by_owner = by_owner.astype(jnp.bfloat16).reshape(owners, layers * cut_len)

    probe_part = jnp.stack([grad_re, grad_im])
    piece_len = probe_part.size // owners
    probe_hi = probe_part.reshape(owners, piece_len).astype(jnp.bfloat16)
    probe_lo = (probe_part.reshape(owners, piece_len) - probe_hi.astype(jnp.float32)).astype(jnp.bfloat16)
    slot_len = layers * cut_len + 2 * piece_len
    slot_len = -(-slot_len // 128) * 128
    outgoing = jnp.concatenate([by_owner, probe_hi, probe_lo], axis=1)
    outgoing = jnp.pad(outgoing, ((0, 0), (0, slot_len - outgoing.shape[1])))
    outgoing = outgoing.reshape(owners, slot_len // 128, 128)
    returned = lax.all_to_all(outgoing, "pos", 0, 0, tiled=True).reshape(owners, slot_len)
    from_owners = returned[:, : layers * cut_len].reshape(owners, layers, cut_len)
    probe_back = returned[:, layers * cut_len : layers * cut_len + 2 * piece_len].astype(jnp.float32)
    probe_row = jnp.sum(probe_back[:, :piece_len], axis=0) + jnp.sum(probe_back[:, piece_len:], axis=0)

    all_r = offsets[:, 0:1] // tile_edge
    all_c = offsets[:, 1:2] // tile_edge
    all_row_in = ((grid_rows >= all_r) & (grid_rows < all_r + tile_span)).astype(jnp.bfloat16)
    all_col_in = ((grid_cols >= all_c) & (grid_cols < all_c + tile_span)).astype(jnp.float32)
    all_found = jnp.sum(
        jnp.dot(all_row_in, local_plus, preferred_element_type=jnp.float32) * all_col_in, axis=1
    ).astype(jnp.int32)
    all_sel = one_hot(jnp.maximum(all_found - 1, 0), tiles_dev, all_found > 0)
    all_sel = all_sel.reshape(owners, layers, tiles_dev)
    my_slice = jnp.einsum("qtk,qtx->kx", all_sel, from_owners, preferred_element_type=jnp.float32)

    probe_cut = jnp.pad(probe_row, (0, cut_len - piece_len))[None]
    gathered = ring_gather(jnp.concatenate([my_slice, probe_cut], axis=0), layers)
    slices = gathered[:, :tiles_dev]
    tile_total = slices.transpose(1, 0, 2).reshape(tiles_dev, layers * cut_len)[:, :tile_px]
    probe_piece = jnp.sum(gathered[:, tiles_dev, :piece_len], axis=0)
    spread = jnp.broadcast_to(probe_piece[None], (owners, piece_len))
    probe_total = lax.all_to_all(spread, "pos", 0, 0, tiled=True).reshape(probe_part.shape)
    return (tile_total.reshape(tiles_dev, n_comps, tile_edge * tile_edge), probe_total)


def ring_gather(values, size, stride=3):
    me = lax.axis_index("tile")
    if size % stride or size <= stride:
        stride = 1
    groups = size // stride

    def shifted(x, shift):
        return lax.ppermute(x, "tile", [(i, (i + shift) % size) for i in range(size)])

    bundle = jnp.stack([values] + [shifted(values, stride * w) for w in range(1, groups)])
    bundles = [bundle]
    source = {(-stride * w) % size: (0, w) for w in range(groups)}
    for r in range(1, stride):
        shift = r if r <= stride // 2 else r - stride
        bundles.append(shifted(bundle, shift))
        for w in range(groups):
            source[(-shift - stride * w) % size] = (r, w)
    by_offset = jnp.stack([bundles[source[d][0]][source[d][1]] for d in range(size)])
    order = (jnp.arange(size, dtype=jnp.int32) - me) % size
    return by_offset[order]


def reduce_probe(probe_part, owners, layers):
    piece_len = probe_part.size // owners
    pieces = probe_part.reshape(owners, piece_len)
    mine = jnp.sum(lax.all_to_all(pieces, "pos", 0, 0, tiled=True), axis=0)
    spread = jnp.broadcast_to(mine[None], (layers, piece_len))
    mine = jnp.sum(lax.all_to_all(spread, "tile", 0, 0, tiled=True), axis=0)
    spread = jnp.broadcast_to(mine[None], (owners, piece_len))
    gathered = lax.all_to_all(spread, "pos", 0, 0, tiled=True)
    return gathered.reshape(probe_part.shape)


def solution(mesh):
    in_specs = (P("pos", None, None), P(), P(), P(), P(("pos", "tile"), None, None))
    out_specs = (P("pos", None, None), P())
    return jax.shard_map(
        per_device, mesh=mesh, in_specs=in_specs, out_specs=out_specs, check_vma=False
    )
```

```python
import math

import jax
import jax.numpy as jnp
from jax import lax
from jax.sharding import PartitionSpec as P

TS = 64
OWN_R = 8


def matmul_hi(left_op, right_op):
    return jnp.dot(
        left_op, right_op, precision=lax.Precision.HIGHEST, preferred_element_type=jnp.float32
    )


def spectral_tables(width_px):
    positions = jnp.arange(width_px, dtype=jnp.int32)
    phase_idx = positions[:, None] * positions[None, :] % width_px
    angles = phase_idx.astype(jnp.float32) * (2.0 * math.pi / width_px)
    norm_factor = 1.0 / math.sqrt(width_px)
    return (jnp.cos(angles) * norm_factor, -jnp.sin(angles) * norm_factor)


def complex_matmul(left_re, left_im, right_re, right_im):
    out_re = matmul_hi(left_re, right_re) - matmul_hi(left_im, right_im)
    out_im = matmul_hi(left_re, right_im) + matmul_hi(left_im, right_re)
    return (out_re, out_im)


def propagation_matrix(width_px, fwd_re, fwd_im, sign_val):
    positions = jnp.arange(width_px, dtype=jnp.int32)
    centred = (positions + width_px // 2) % width_px - width_px // 2
    angles = (centred * centred).astype(jnp.float32) * (-0.2 / width_px) * sign_val
    phase_re = jnp.cos(angles)[:, None]
    phase_im = jnp.sin(angles)[:, None]
    scaled_re = phase_re * fwd_re - phase_im * fwd_im
    scaled_im = phase_re * fwd_im + phase_im * fwd_re
    return complex_matmul(fwd_re, -fwd_im, scaled_re, scaled_im)


def stacked_table(table_re, table_im):
    column = jnp.concatenate([table_re, table_im], axis=0)
    block = jnp.concatenate(
        [jnp.concatenate([table_re, -table_im], axis=1), jnp.concatenate([table_im, table_re], axis=1)],
        axis=0,
    )
    return column, block


def transform(part_re, part_im, table):
    column, block = table
    left = jnp.concatenate(
        [jnp.concatenate([part_re, -part_im], axis=1), jnp.concatenate([part_im, part_re], axis=1)],
        axis=0,
    )
    mid = matmul_hi(left, column)
    out = matmul_hi(block, mid)
    width = part_re.shape[0]
    return out[:width], out[width:]


def product(left_re, left_im, right_re, right_im):
    return (left_re * right_re - left_im * right_im, left_re * right_im + left_im * right_re)


def one_hot(index, size, live=None):
    hit = index[:, None] == jnp.arange(size, dtype=index.dtype)[None, :]
    if live is not None:
        hit = hit & live[:, None]
    return hit.astype(jnp.bfloat16)


def per_device(obj_tiles, tile_map, offsets, probe, intens):
    owners = lax.axis_size("pos")
    layers = lax.axis_size("tile")
    me_pos = lax.axis_index("pos")
    me_tile = lax.axis_index("tile")
    tiles_dev = obj_tiles.shape[0]
    n_comps = obj_tiles.shape[1]
    tile_edge = TS
    width_px = probe.shape[-1]
    tile_span = width_px // tile_edge + 1
    own_c = owners // OWN_R
    grid_r, grid_c = tile_map.shape
    span_idx = jnp.arange(tile_span, dtype=jnp.int32)

    mine = (tile_map // tiles_dev) == me_pos
    local_plus = jnp.where(mine, tile_map - me_pos * tiles_dev + 1, 0).astype(jnp.bfloat16)
    by_device = offsets.reshape(owners, layers, 2)
    peer_corners = lax.dynamic_index_in_dim(by_device, me_tile, 1, keepdims=False)
    peer_r = peer_corners[:, 0:1] // tile_edge
    peer_c = peer_corners[:, 1:2] // tile_edge
    grid_rows = jnp.arange(grid_r, dtype=jnp.int32)[None, :]
    grid_cols = jnp.arange(grid_c, dtype=jnp.int32)[None, :]
    row_in = ((grid_rows >= peer_r) & (grid_rows < peer_r + tile_span)).astype(jnp.bfloat16)
    col_in = ((grid_cols >= peer_c) & (grid_cols < peer_c + tile_span)).astype(jnp.float32)
    by_col = jnp.dot(row_in, local_plus, preferred_element_type=jnp.float32)
    found = jnp.sum(by_col * col_in, axis=1).astype(jnp.int32)
    send_live = found > 0
    send_local = jnp.maximum(found - 1, 0)
    chosen = obj_tiles[send_local]

    my_corner = lax.dynamic_index_in_dim(offsets, me_pos * layers + me_tile, 0, keepdims=False)
    row_ids = my_corner[0] // tile_edge + span_idx
    col_ids = my_corner[1] // tile_edge + span_idx
    my_owner = (tile_map[row_ids[:, None], col_ids[None, :]] // tiles_dev).reshape(-1)
    inner_y = my_corner[0] % tile_edge
    inner_x = my_corner[1] % tile_edge
    zero_idx = jnp.zeros((), jnp.int32)
    fwd_re, fwd_im = spectral_tables(width_px)
    ahead_re, ahead_im = propagation_matrix(width_px, fwd_re, fwd_im, 1.0)
    behind_re, behind_im = propagation_matrix(width_px, fwd_re, fwd_im, -1.0)
    ahead = stacked_table(ahead_re, ahead_im)
    forward = stacked_table(fwd_re, fwd_im)
    backward = stacked_table(fwd_re, -fwd_im)
    behind = stacked_table(behind_re, behind_im)
    probe_re = probe[0]
    probe_im = probe[1]
    received = lax.all_to_all(chosen, "pos", split_axis=0, concat_axis=0, tiled=True)
    pieces = received[my_owner]
    region = pieces.reshape(tile_span, tile_span, n_comps, tile_edge, tile_edge).transpose(
        2, 0, 3, 1, 4
    )
    region = region.reshape(n_comps, tile_span * tile_edge, tile_span * tile_edge)
    patch_px = lax.dynamic_slice(
        region, (zero_idx, inner_y, inner_x), (n_comps, width_px, width_px)
    )
    fetched = patch_px.astype(jnp.float32)
    entry_patch = fetched[:2]
    leaving = fetched[2:]
    first_re, first_im = product(probe_re, probe_im, entry_patch[0], entry_patch[1])
    spread_re, spread_im = transform(first_re, first_im, ahead)
    second_re, second_im = product(spread_re, spread_im, leaving[0], leaving[1])
    far_re, far_im = transform(second_re, second_im, forward)
    excess = far_re * far_re + far_im * far_im - intens[0]
    back_re, back_im = transform(excess * far_re, excess * far_im, backward)
    exit_re, exit_im = product(spread_re, -spread_im, back_re, back_im)
    mid_re, mid_im = product(leaving[0], -leaving[1], back_re, back_im)
    inner_re, inner_im = transform(mid_re, mid_im, behind)
    entry_re, entry_im = product(probe_re, -probe_im, inner_re, inner_im)
    grad_re, grad_im = product(entry_patch[0], -entry_patch[1], inner_re, inner_im)
    patch_grad = jnp.stack([entry_re, entry_im, exit_re, exit_im]).astype(jnp.bfloat16)

    region_px = tile_span * tile_edge
    shift_y = one_hot(jnp.arange(region_px, dtype=jnp.int32) - inner_y, width_px)
    shift_x = one_hot(jnp.arange(region_px, dtype=jnp.int32) - inner_x, width_px)
    shift_y = shift_y.reshape(tile_span, tile_edge, width_px)
    shift_x = shift_x.reshape(tile_span, tile_edge, width_px)
    rows_cut = jnp.einsum("irk,ckm->cirm", shift_y, patch_grad, preferred_element_type=jnp.float32)
    rows_cut = rows_cut.astype(jnp.bfloat16)
    tiles_cut = jnp.einsum("cirm,jsm->ijcrs", rows_cut, shift_x, preferred_element_type=jnp.float32)
    n_foot = tile_span * tile_span
    tile_px = n_comps * tile_edge * tile_edge
    tiles_cut = tiles_cut.astype(jnp.bfloat16).reshape(n_foot, tile_px)

    cut_len = -(-tile_px // layers)
    cut_len = -(-cut_len // 128) * 128
    pad_px = cut_len * layers - tile_px
    cut = jnp.pad(tiles_cut, ((0, 0), (0, pad_px))).reshape(n_foot, layers, cut_len)
    cut = cut.transpose(1, 0, 2).reshape(layers, n_foot, cut_len // 128, 128)
    from_column = lax.all_to_all(cut, "tile", 0, 0, tiled=True)
    from_column = from_column.reshape(layers, n_foot, cut_len)

    col_corners = lax.dynamic_index_in_dim(by_device, me_pos, 0, keepdims=False)
    col_rows = col_corners[:, 0:1] // tile_edge + span_idx[None, :]
    col_cols = col_corners[:, 1:2] // tile_edge + span_idx[None, :]
    col_owner = tile_map[col_rows[:, :, None], col_cols[:, None, :]].reshape(layers, n_foot)
    col_owner = col_owner // tiles_dev
    to_owner = (col_owner[:, :, None] == jnp.arange(owners)[None, None, :]).astype(jnp.bfloat16)
    by_owner = jnp.einsum("tsp,tsx->ptx", to_owner, from_column, preferred_element_type=jnp.float32)
    by_owner = by_owner.astype(jnp.bfloat16).reshape(owners, layers * cut_len)

    probe_part = jnp.stack([grad_re, grad_im])
    piece_len = probe_part.size // owners
    probe_hi = probe_part.reshape(owners, piece_len).astype(jnp.bfloat16)
    probe_lo = (probe_part.reshape(owners, piece_len) - probe_hi.astype(jnp.float32)).astype(jnp.bfloat16)
    slot_len = layers * cut_len + 2 * piece_len
    slot_len = -(-slot_len // 128) * 128
    outgoing = jnp.concatenate([by_owner, probe_hi, probe_lo], axis=1)
    outgoing = jnp.pad(outgoing, ((0, 0), (0, slot_len - outgoing.shape[1])))
    outgoing = outgoing.reshape(owners, slot_len // 128, 128)
    returned = lax.all_to_all(outgoing, "pos", 0, 0, tiled=True).reshape(owners, slot_len)
    from_owners = returned[:, : layers * cut_len].reshape(owners, layers, cut_len)
    probe_back = returned[:, layers * cut_len : layers * cut_len + 2 * piece_len].astype(jnp.float32)
    probe_row = jnp.sum(probe_back[:, :piece_len], axis=0) + jnp.sum(probe_back[:, piece_len:], axis=0)

    all_r = offsets[:, 0:1] // tile_edge
    all_c = offsets[:, 1:2] // tile_edge
    all_row_in = ((grid_rows >= all_r) & (grid_rows < all_r + tile_span)).astype(jnp.bfloat16)
    all_col_in = ((grid_cols >= all_c) & (grid_cols < all_c + tile_span)).astype(jnp.float32)
    all_found = jnp.sum(
        jnp.dot(all_row_in, local_plus, preferred_element_type=jnp.float32) * all_col_in, axis=1
    ).astype(jnp.int32)
    all_sel = one_hot(jnp.maximum(all_found - 1, 0), tiles_dev, all_found > 0)
    all_sel = all_sel.reshape(owners, layers, tiles_dev)
    my_slice = jnp.einsum("qtk,qtx->kx", all_sel, from_owners, preferred_element_type=jnp.float32)

    probe_cut = jnp.pad(probe_row, (0, cut_len - piece_len))[None]
    by_offset = ring_pieces(jnp.concatenate([my_slice, probe_cut], axis=0), layers)
    flat = jnp.concatenate(by_offset, axis=1)
    start = (layers - me_tile) % layers * cut_len
    ordered = lax.dynamic_slice_in_dim(jnp.concatenate([flat, flat], axis=1), start, layers * cut_len, 1)
    tile_total = ordered[:tiles_dev, :tile_px]
    probe_piece = jnp.sum(ordered[tiles_dev].reshape(layers, cut_len)[:, :piece_len], axis=0)
    spread = jnp.broadcast_to(probe_piece[None], (owners, piece_len))
    probe_total = lax.all_to_all(spread, "pos", 0, 0, tiled=True).reshape(probe_part.shape)
    return (tile_total.reshape(tiles_dev, n_comps, tile_edge * tile_edge), probe_total)


def ring_pieces(values, size):
    to_right = [(i, (i + 1) % size) for i in range(size)]
    to_left = [(i, (i - 1) % size) for i in range(size)]
    back = [values]
    ahead = []
    going_right = values
    going_left = values
    for step in range(1, size // 2 + 1):
        going_right = lax.ppermute(going_right, "tile", to_right)
        back.append(going_right)
        if step < size - size // 2:
            going_left = lax.ppermute(going_left, "tile", to_left)
            ahead.append(going_left)
    return [back[0]] + ahead + [back[size - d] for d in range(len(ahead) + 1, size)]


def reduce_probe(probe_part, owners, layers):
    piece_len = probe_part.size // owners
    pieces = probe_part.reshape(owners, piece_len)
    mine = jnp.sum(lax.all_to_all(pieces, "pos", 0, 0, tiled=True), axis=0)
    spread = jnp.broadcast_to(mine[None], (layers, piece_len))
    mine = jnp.sum(lax.all_to_all(spread, "tile", 0, 0, tiled=True), axis=0)
    spread = jnp.broadcast_to(mine[None], (owners, piece_len))
    gathered = lax.all_to_all(spread, "pos", 0, 0, tiled=True)
    return gathered.reshape(probe_part.shape)


def solution(mesh):
    in_specs = (P("pos", None, None), P(), P(), P(), P(("pos", "tile"), None, None))
    out_specs = (P("pos", None, None), P())
    return jax.shard_map(
        per_device, mesh=mesh, in_specs=in_specs, out_specs=out_specs, check_vma=False
    )
```

```python
import math

import jax
import jax.numpy as jnp
from jax import lax
from jax.sharding import PartitionSpec as P

TS = 64
OWN_R = 8


def matmul_hi(left_op, right_op):
    return jnp.dot(
        left_op, right_op, precision=lax.Precision.HIGHEST, preferred_element_type=jnp.float32
    )


def spectral_tables(width_px):
    positions = jnp.arange(width_px, dtype=jnp.int32)
    phase_idx = positions[:, None] * positions[None, :] % width_px
    angles = phase_idx.astype(jnp.float32) * (2.0 * math.pi / width_px)
    norm_factor = 1.0 / math.sqrt(width_px)
    return (jnp.cos(angles) * norm_factor, -jnp.sin(angles) * norm_factor)


def complex_matmul(left_re, left_im, right_re, right_im):
    out_re = matmul_hi(left_re, right_re) - matmul_hi(left_im, right_im)
    out_im = matmul_hi(left_re, right_im) + matmul_hi(left_im, right_re)
    return (out_re, out_im)


def propagation_matrix(width_px, fwd_re, fwd_im, sign_val):
    positions = jnp.arange(width_px, dtype=jnp.int32)
    centred = (positions + width_px // 2) % width_px - width_px // 2
    angles = (centred * centred).astype(jnp.float32) * (-0.2 / width_px) * sign_val
    phase_re = jnp.cos(angles)[:, None]
    phase_im = jnp.sin(angles)[:, None]
    scaled_re = phase_re * fwd_re - phase_im * fwd_im
    scaled_im = phase_re * fwd_im + phase_im * fwd_re
    return complex_matmul(fwd_re, -fwd_im, scaled_re, scaled_im)


def stacked_table(table_re, table_im):
    column = jnp.concatenate([table_re, table_im], axis=0)
    block = jnp.concatenate(
        [jnp.concatenate([table_re, -table_im], axis=1), jnp.concatenate([table_im, table_re], axis=1)],
        axis=0,
    )
    return column, block


def transform(part_re, part_im, table):
    column, block = table
    left = jnp.concatenate(
        [jnp.concatenate([part_re, -part_im], axis=1), jnp.concatenate([part_im, part_re], axis=1)],
        axis=0,
    )
    mid = matmul_hi(left, column)
    out = matmul_hi(block, mid)
    width = part_re.shape[0]
    return out[:width], out[width:]


def product(left_re, left_im, right_re, right_im):
    return (left_re * right_re - left_im * right_im, left_re * right_im + left_im * right_re)


def one_hot(index, size, live=None):
    hit = index[:, None] == jnp.arange(size, dtype=index.dtype)[None, :]
    if live is not None:
        hit = hit & live[:, None]
    return hit.astype(jnp.bfloat16)


def per_device(obj_tiles, tile_map, offsets, probe, intens):
    owners = lax.axis_size("pos")
    layers = lax.axis_size("tile")
    me_pos = lax.axis_index("pos")
    me_tile = lax.axis_index("tile")
    tiles_dev = obj_tiles.shape[0]
    n_comps = obj_tiles.shape[1]
    tile_edge = TS
    width_px = probe.shape[-1]
    tile_span = width_px // tile_edge + 1
    own_c = owners // OWN_R
    grid_r, grid_c = tile_map.shape
    span_idx = jnp.arange(tile_span, dtype=jnp.int32)

    mine = (tile_map // tiles_dev) == me_pos
    local_plus = jnp.where(mine, tile_map - me_pos * tiles_dev + 1, 0).astype(jnp.bfloat16)
    by_device = offsets.reshape(owners, layers, 2)
    peer_corners = lax.dynamic_index_in_dim(by_device, me_tile, 1, keepdims=False)
    peer_r = peer_corners[:, 0:1] // tile_edge
    peer_c = peer_corners[:, 1:2] // tile_edge
    grid_rows = jnp.arange(grid_r, dtype=jnp.int32)[None, :]
    grid_cols = jnp.arange(grid_c, dtype=jnp.int32)[None, :]
    row_in = ((grid_rows >= peer_r) & (grid_rows < peer_r + tile_span)).astype(jnp.bfloat16)
    col_in = ((grid_cols >= peer_c) & (grid_cols < peer_c + tile_span)).astype(jnp.float32)
    by_col = jnp.dot(row_in, local_plus, preferred_element_type=jnp.float32)
    found = jnp.sum(by_col * col_in, axis=1).astype(jnp.int32)
    send_live = found > 0
    send_local = jnp.maximum(found - 1, 0)
    chosen = obj_tiles[send_local]

    my_corner = lax.dynamic_index_in_dim(offsets, me_pos * layers + me_tile, 0, keepdims=False)
    row_ids = my_corner[0] // tile_edge + span_idx
    col_ids = my_corner[1] // tile_edge + span_idx
    my_owner = (tile_map[row_ids[:, None], col_ids[None, :]] // tiles_dev).reshape(-1)
    inner_y = my_corner[0] % tile_edge
    inner_x = my_corner[1] % tile_edge
    zero_idx = jnp.zeros((), jnp.int32)
    fwd_re, fwd_im = spectral_tables(width_px)
    ahead_re, ahead_im = propagation_matrix(width_px, fwd_re, fwd_im, 1.0)
    behind_re, behind_im = propagation_matrix(width_px, fwd_re, fwd_im, -1.0)
    ahead = stacked_table(ahead_re, ahead_im)
    forward = stacked_table(fwd_re, fwd_im)
    backward = stacked_table(fwd_re, -fwd_im)
    behind = stacked_table(behind_re, behind_im)
    probe_re = probe[0]
    probe_im = probe[1]
    received = lax.all_to_all(chosen, "pos", split_axis=0, concat_axis=0, tiled=True)
    pieces = received[my_owner]
    region = pieces.reshape(tile_span, tile_span, n_comps, tile_edge, tile_edge).transpose(
        2, 0, 3, 1, 4
    )
    region = region.reshape(n_comps, tile_span * tile_edge, tile_span * tile_edge)
    patch_px = lax.dynamic_slice(
        region, (zero_idx, inner_y, inner_x), (n_comps, width_px, width_px)
    )
    fetched = patch_px.astype(jnp.float32)
    entry_patch = fetched[:2]
    leaving = fetched[2:]
    first_re, first_im = product(probe_re, probe_im, entry_patch[0], entry_patch[1])
    spread_re, spread_im = transform(first_re, first_im, ahead)
    second_re, second_im = product(spread_re, spread_im, leaving[0], leaving[1])
    far_re, far_im = transform(second_re, second_im, forward)
    excess = far_re * far_re + far_im * far_im - intens[0]
    back_re, back_im = transform(excess * far_re, excess * far_im, backward)
    exit_re, exit_im = product(spread_re, -spread_im, back_re, back_im)
    mid_re, mid_im = product(leaving[0], -leaving[1], back_re, back_im)
    inner_re, inner_im = transform(mid_re, mid_im, behind)
    entry_re, entry_im = product(probe_re, -probe_im, inner_re, inner_im)
    grad_re, grad_im = product(entry_patch[0], -entry_patch[1], inner_re, inner_im)
    patch_grad = jnp.stack([entry_re, entry_im, exit_re, exit_im]).astype(jnp.bfloat16)

    region_px = tile_span * tile_edge
    shift_y = one_hot(jnp.arange(region_px, dtype=jnp.int32) - inner_y, width_px)
    shift_x = one_hot(jnp.arange(region_px, dtype=jnp.int32) - inner_x, width_px)
    shift_y = shift_y.reshape(tile_span, tile_edge, width_px)
    shift_x = shift_x.reshape(tile_span, tile_edge, width_px)
    rows_cut = jnp.einsum("irk,ckm->cirm", shift_y, patch_grad, preferred_element_type=jnp.float32)
    rows_cut = rows_cut.astype(jnp.bfloat16)
    tiles_cut = jnp.einsum("cirm,jsm->ijcrs", rows_cut, shift_x, preferred_element_type=jnp.float32)
    n_foot = tile_span * tile_span
    tile_px = n_comps * tile_edge * tile_edge
    tiles_cut = tiles_cut.astype(jnp.bfloat16).reshape(n_foot, tile_px)

    cut_len = -(-tile_px // layers)
    cut_len = -(-cut_len // 128) * 128
    pad_px = cut_len * layers - tile_px
    cut = jnp.pad(tiles_cut, ((0, 0), (0, pad_px))).reshape(n_foot, layers, cut_len)
    cut = cut.transpose(1, 0, 2).reshape(layers, n_foot * cut_len // 128, 128)
    from_column = lax.all_to_all(cut, "tile", 0, 0, tiled=True)
    from_column = from_column.reshape(layers, n_foot, cut_len)

    col_corners = lax.dynamic_index_in_dim(by_device, me_pos, 0, keepdims=False)
    col_rows = col_corners[:, 0:1] // tile_edge + span_idx[None, :]
    col_cols = col_corners[:, 1:2] // tile_edge + span_idx[None, :]
    col_owner = tile_map[col_rows[:, :, None], col_cols[:, None, :]].reshape(layers, n_foot)
    col_owner = col_owner // tiles_dev
    to_owner = (col_owner[:, :, None] == jnp.arange(owners)[None, None, :]).astype(jnp.bfloat16)
    by_owner = jnp.einsum("tsp,tsx->ptx", to_owner, from_column, preferred_element_type=jnp.float32)
    by_owner = by_owner.astype(jnp.bfloat16).reshape(owners, layers * cut_len)

    probe_part = jnp.stack([grad_re, grad_im])
    piece_len = probe_part.size // owners
    probe_hi = probe_part.reshape(owners, piece_len).astype(jnp.bfloat16)
    probe_lo = (probe_part.reshape(owners, piece_len) - probe_hi.astype(jnp.float32)).astype(jnp.bfloat16)
    slot_len = layers * cut_len + 2 * piece_len
    slot_len = -(-slot_len // 128) * 128
    outgoing = jnp.concatenate([by_owner, probe_hi, probe_lo], axis=1)
    outgoing = jnp.pad(outgoing, ((0, 0), (0, slot_len - outgoing.shape[1])))
    outgoing = outgoing.reshape(owners, slot_len // 128, 128)
    returned = lax.all_to_all(outgoing, "pos", 0, 0, tiled=True).reshape(owners, slot_len)
    from_owners = returned[:, : layers * cut_len].reshape(owners, layers, cut_len)
    probe_back = returned[:, layers * cut_len : layers * cut_len + 2 * piece_len].astype(jnp.float32)
    probe_row = jnp.sum(probe_back[:, :piece_len], axis=0) + jnp.sum(probe_back[:, piece_len:], axis=0)

    all_r = offsets[:, 0:1] // tile_edge
    all_c = offsets[:, 1:2] // tile_edge
    all_row_in = ((grid_rows >= all_r) & (grid_rows < all_r + tile_span)).astype(jnp.bfloat16)
    all_col_in = ((grid_cols >= all_c) & (grid_cols < all_c + tile_span)).astype(jnp.float32)
    all_found = jnp.sum(
        jnp.dot(all_row_in, local_plus, preferred_element_type=jnp.float32) * all_col_in, axis=1
    ).astype(jnp.int32)
    all_sel = one_hot(jnp.maximum(all_found - 1, 0), tiles_dev, all_found > 0)
    all_sel = all_sel.reshape(owners, layers, tiles_dev)
    my_slice = jnp.einsum("qtk,qtx->kx", all_sel, from_owners, preferred_element_type=jnp.float32)

    probe_cut = jnp.pad(probe_row, (0, cut_len - piece_len))[None]
    gathered = ring_gather(jnp.concatenate([my_slice, probe_cut], axis=0), layers)
    slices = gathered[:, :tiles_dev]
    tile_total = slices.transpose(1, 0, 2).reshape(tiles_dev, layers * cut_len)[:, :tile_px]
    probe_piece = jnp.sum(gathered[:, tiles_dev, :piece_len], axis=0)
    spread = jnp.broadcast_to(probe_piece[None], (owners, piece_len))
    probe_total = lax.all_to_all(spread, "pos", 0, 0, tiled=True).reshape(probe_part.shape)
    return (tile_total.reshape(tiles_dev, n_comps, tile_edge * tile_edge), probe_total)


def ring_gather(values, size):
    me = lax.axis_index("tile")
    to_right = [(i, (i + 1) % size) for i in range(size)]
    to_left = [(i, (i - 1) % size) for i in range(size)]
    back = [values]
    ahead = []
    going_right = values
    going_left = values
    for step in range(1, size // 2 + 1):
        going_right = lax.ppermute(going_right, "tile", to_right)
        back.append(going_right)
        if step < size - size // 2:
            going_left = lax.ppermute(going_left, "tile", to_left)
            ahead.append(going_left)
    by_offset = [back[0]] + ahead + [back[size - d] for d in range(len(ahead) + 1, size)]
    order = (jnp.arange(size, dtype=jnp.int32) - me) % size
    return jnp.stack(by_offset)[order]


def reduce_probe(probe_part, owners, layers):
    piece_len = probe_part.size // owners
    pieces = probe_part.reshape(owners, piece_len)
    mine = jnp.sum(lax.all_to_all(pieces, "pos", 0, 0, tiled=True), axis=0)
    spread = jnp.broadcast_to(mine[None], (layers, piece_len))
    mine = jnp.sum(lax.all_to_all(spread, "tile", 0, 0, tiled=True), axis=0)
    spread = jnp.broadcast_to(mine[None], (owners, piece_len))
    gathered = lax.all_to_all(spread, "pos", 0, 0, tiled=True)
    return gathered.reshape(probe_part.shape)


def solution(mesh):
    in_specs = (P("pos", None, None), P(), P(), P(), P(("pos", "tile"), None, None))
    out_specs = (P("pos", None, None), P())
    return jax.shard_map(
        per_device, mesh=mesh, in_specs=in_specs, out_specs=out_specs, check_vma=False
    )
```

```python
import math

import jax
import jax.numpy as jnp
from jax import lax
from jax.sharding import PartitionSpec as P

TS = 64
OWN_R = 8


def matmul_hi(left_op, right_op):
    return jnp.dot(
        left_op, right_op, precision=lax.Precision.HIGHEST, preferred_element_type=jnp.float32
    )


def spectral_tables(width_px):
    positions = jnp.arange(width_px, dtype=jnp.int32)
    phase_idx = positions[:, None] * positions[None, :] % width_px
    angles = phase_idx.astype(jnp.float32) * (2.0 * math.pi / width_px)
    norm_factor = 1.0 / math.sqrt(width_px)
    return (jnp.cos(angles) * norm_factor, -jnp.sin(angles) * norm_factor)


def complex_matmul(left_re, left_im, right_re, right_im):
    out_re = matmul_hi(left_re, right_re) - matmul_hi(left_im, right_im)
    out_im = matmul_hi(left_re, right_im) + matmul_hi(left_im, right_re)
    return (out_re, out_im)


def propagation_matrix(width_px, fwd_re, fwd_im, sign_val):
    positions = jnp.arange(width_px, dtype=jnp.int32)
    centred = (positions + width_px // 2) % width_px - width_px // 2
    angles = (centred * centred).astype(jnp.float32) * (-0.2 / width_px) * sign_val
    phase_re = jnp.cos(angles)[:, None]
    phase_im = jnp.sin(angles)[:, None]
    scaled_re = phase_re * fwd_re - phase_im * fwd_im
    scaled_im = phase_re * fwd_im + phase_im * fwd_re
    return complex_matmul(fwd_re, -fwd_im, scaled_re, scaled_im)


def stacked_table(table_re, table_im):
    column = jnp.concatenate([table_re, table_im], axis=0)
    block = jnp.concatenate(
        [jnp.concatenate([table_re, -table_im], axis=1), jnp.concatenate([table_im, table_re], axis=1)],
        axis=0,
    )
    return column, block


def transform(part_re, part_im, table):
    column, block = table
    left = jnp.concatenate(
        [jnp.concatenate([part_re, -part_im], axis=1), jnp.concatenate([part_im, part_re], axis=1)],
        axis=0,
    )
    mid = matmul_hi(left, column)
    out = matmul_hi(block, mid)
    width = part_re.shape[0]
    return out[:width], out[width:]


def product(left_re, left_im, right_re, right_im):
    return (left_re * right_re - left_im * right_im, left_re * right_im + left_im * right_re)


def one_hot(index, size, live=None):
    hit = index[:, None] == jnp.arange(size, dtype=index.dtype)[None, :]
    if live is not None:
        hit = hit & live[:, None]
    return hit.astype(jnp.bfloat16)


def per_device(obj_tiles, tile_map, offsets, probe, intens):
    owners = lax.axis_size("pos")
    layers = lax.axis_size("tile")
    me_pos = lax.axis_index("pos")
    me_tile = lax.axis_index("tile")
    tiles_dev = obj_tiles.shape[0]
    n_comps = obj_tiles.shape[1]
    tile_edge = TS
    width_px = probe.shape[-1]
    tile_span = width_px // tile_edge + 1
    own_c = owners // OWN_R
    grid_r, grid_c = tile_map.shape
    span_idx = jnp.arange(tile_span, dtype=jnp.int32)

    mine = (tile_map // tiles_dev) == me_pos
    local_plus = jnp.where(mine, tile_map - me_pos * tiles_dev + 1, 0).astype(jnp.bfloat16)
    by_device = offsets.reshape(owners, layers, 2)
    peer_corners = lax.dynamic_index_in_dim(by_device, me_tile, 1, keepdims=False)
    peer_r = peer_corners[:, 0:1] // tile_edge
    peer_c = peer_corners[:, 1:2] // tile_edge
    grid_rows = jnp.arange(grid_r, dtype=jnp.int32)[None, :]
    grid_cols = jnp.arange(grid_c, dtype=jnp.int32)[None, :]
    row_in = ((grid_rows >= peer_r) & (grid_rows < peer_r + tile_span)).astype(jnp.bfloat16)
    col_in = ((grid_cols >= peer_c) & (grid_cols < peer_c + tile_span)).astype(jnp.float32)
    by_col = jnp.dot(row_in, local_plus, preferred_element_type=jnp.float32)
    found = jnp.sum(by_col * col_in, axis=1).astype(jnp.int32)
    send_live = found > 0
    send_local = jnp.maximum(found - 1, 0)
    chosen = obj_tiles[send_local]

    my_corner = lax.dynamic_index_in_dim(offsets, me_pos * layers + me_tile, 0, keepdims=False)
    row_ids = my_corner[0] // tile_edge + span_idx
    col_ids = my_corner[1] // tile_edge + span_idx
    my_owner = (tile_map[row_ids[:, None], col_ids[None, :]] // tiles_dev).reshape(-1)
    inner_y = my_corner[0] % tile_edge
    inner_x = my_corner[1] % tile_edge
    zero_idx = jnp.zeros((), jnp.int32)
    fwd_re, fwd_im = spectral_tables(width_px)
    ahead_re, ahead_im = propagation_matrix(width_px, fwd_re, fwd_im, 1.0)
    behind_re, behind_im = propagation_matrix(width_px, fwd_re, fwd_im, -1.0)
    ahead = stacked_table(ahead_re, ahead_im)
    forward = stacked_table(fwd_re, fwd_im)
    backward = stacked_table(fwd_re, -fwd_im)
    behind = stacked_table(behind_re, behind_im)
    probe_re = probe[0]
    probe_im = probe[1]
    received = lax.all_to_all(chosen, "pos", split_axis=0, concat_axis=0, tiled=True)
    pieces = received[my_owner]
    region = pieces.reshape(tile_span, tile_span, n_comps, tile_edge, tile_edge).transpose(
        2, 0, 3, 1, 4
    )
    region = region.reshape(n_comps, tile_span * tile_edge, tile_span * tile_edge)
    patch_px = lax.dynamic_slice(
        region, (zero_idx, inner_y, inner_x), (n_comps, width_px, width_px)
    )
    fetched = patch_px.astype(jnp.float32)
    entry_patch = fetched[:2]
    leaving = fetched[2:]
    first_re, first_im = product(probe_re, probe_im, entry_patch[0], entry_patch[1])
    spread_re, spread_im = transform(first_re, first_im, ahead)
    second_re, second_im = product(spread_re, spread_im, leaving[0], leaving[1])
    far_re, far_im = transform(second_re, second_im, forward)
    excess = far_re * far_re + far_im * far_im - intens[0]
    back_re, back_im = transform(excess * far_re, excess * far_im, backward)
    exit_re, exit_im = product(spread_re, -spread_im, back_re, back_im)
    mid_re, mid_im = product(leaving[0], -leaving[1], back_re, back_im)
    inner_re, inner_im = transform(mid_re, mid_im, behind)
    entry_re, entry_im = product(probe_re, -probe_im, inner_re, inner_im)
    grad_re, grad_im = product(entry_patch[0], -entry_patch[1], inner_re, inner_im)
    patch_grad = jnp.stack([entry_re, entry_im, exit_re, exit_im]).astype(jnp.bfloat16)

    region_px = tile_span * tile_edge
    shift_y = one_hot(jnp.arange(region_px, dtype=jnp.int32) - inner_y, width_px)
    shift_x = one_hot(jnp.arange(region_px, dtype=jnp.int32) - inner_x, width_px)
    shift_y = shift_y.reshape(tile_span, tile_edge, width_px)
    shift_x = shift_x.reshape(tile_span, tile_edge, width_px)
    rows_cut = jnp.einsum("irk,ckm->cirm", shift_y, patch_grad, preferred_element_type=jnp.float32)
    rows_cut = rows_cut.astype(jnp.bfloat16)
    tiles_cut = jnp.einsum("cirm,jsm->ijcrs", rows_cut, shift_x, preferred_element_type=jnp.float32)
    n_foot = tile_span * tile_span
    tile_px = n_comps * tile_edge * tile_edge
    tiles_cut = tiles_cut.astype(jnp.bfloat16).reshape(n_foot, tile_px)

    cut_len = -(-tile_px // layers)
    cut_len = -(-cut_len // 128) * 128
    pad_px = cut_len * layers - tile_px
    cut = jnp.pad(tiles_cut, ((0, 0), (0, pad_px))).reshape(n_foot, layers, cut_len)
    cut = cut.transpose(1, 0, 2).reshape(layers, n_foot * cut_len // 128, 128)
    from_column = lax.all_to_all(cut, "tile", 0, 0, tiled=True)
    from_column = from_column.reshape(layers, n_foot, cut_len)

    col_corners = lax.dynamic_index_in_dim(by_device, me_pos, 0, keepdims=False)
    col_rows = col_corners[:, 0:1] // tile_edge + span_idx[None, :]
    col_cols = col_corners[:, 1:2] // tile_edge + span_idx[None, :]
    col_owner = tile_map[col_rows[:, :, None], col_cols[:, None, :]].reshape(layers, n_foot)
    col_owner = col_owner // tiles_dev
    to_owner = (col_owner[:, :, None] == jnp.arange(owners)[None, None, :]).astype(jnp.bfloat16)
    by_owner = jnp.einsum("tsp,tsx->ptx", to_owner, from_column, preferred_element_type=jnp.float32)
    by_owner = by_owner.astype(jnp.bfloat16).reshape(owners, layers * cut_len)

    probe_part = jnp.stack([grad_re, grad_im])
    piece_len = probe_part.size // owners
    probe_hi = probe_part.reshape(owners, piece_len).astype(jnp.bfloat16)
    probe_lo = (probe_part.reshape(owners, piece_len) - probe_hi.astype(jnp.float32)).astype(jnp.bfloat16)
    slot_len = layers * cut_len + 2 * piece_len
    slot_len = -(-slot_len // 128) * 128
    outgoing = jnp.concatenate([by_owner, probe_hi, probe_lo], axis=1)
    outgoing = jnp.pad(outgoing, ((0, 0), (0, slot_len - outgoing.shape[1])))
    outgoing = outgoing.reshape(owners, slot_len // 128, 128)
    returned = lax.all_to_all(outgoing, "pos", 0, 0, tiled=True).reshape(owners, slot_len)
    from_owners = returned[:, : layers * cut_len].reshape(owners, layers, cut_len)
    probe_back = returned[:, layers * cut_len : layers * cut_len + 2 * piece_len].astype(jnp.float32)
    probe_row = jnp.sum(probe_back[:, :piece_len], axis=0) + jnp.sum(probe_back[:, piece_len:], axis=0)

    all_r = offsets[:, 0:1] // tile_edge
    all_c = offsets[:, 1:2] // tile_edge
    all_row_in = ((grid_rows >= all_r) & (grid_rows < all_r + tile_span)).astype(jnp.bfloat16)
    all_col_in = ((grid_cols >= all_c) & (grid_cols < all_c + tile_span)).astype(jnp.float32)
    all_found = jnp.sum(
        jnp.dot(all_row_in, local_plus, preferred_element_type=jnp.float32) * all_col_in, axis=1
    ).astype(jnp.int32)
    all_sel = one_hot(jnp.maximum(all_found - 1, 0), tiles_dev, all_found > 0)
    all_sel = all_sel.reshape(owners, layers, tiles_dev)
    my_slice = jnp.einsum("qtk,qtx->kx", all_sel, from_owners, preferred_element_type=jnp.float32)

    probe_cut = jnp.pad(probe_row, (0, cut_len - piece_len))[None]
    block = jnp.concatenate([my_slice, probe_cut], axis=0)
    gathered = ring_gather(block.reshape(-1, 128), layers).reshape((layers,) + block.shape)
    slices = gathered[:, :tiles_dev]
    tile_total = slices.transpose(1, 0, 2).reshape(tiles_dev, layers * cut_len)[:, :tile_px]
    probe_piece = jnp.sum(gathered[:, tiles_dev, :piece_len], axis=0)
    spread = jnp.broadcast_to(probe_piece[None], (owners, piece_len))
    probe_total = lax.all_to_all(spread, "pos", 0, 0, tiled=True).reshape(probe_part.shape)
    return (tile_total.reshape(tiles_dev, n_comps, tile_edge * tile_edge), probe_total)


def ring_gather(values, size):
    me = lax.axis_index("tile")
    to_right = [(i, (i + 1) % size) for i in range(size)]
    to_left = [(i, (i - 1) % size) for i in range(size)]
    back = [values]
    ahead = []
    going_right = values
    going_left = values
    for step in range(1, size // 2 + 1):
        going_right = lax.ppermute(going_right, "tile", to_right)
        back.append(going_right)
        if step < size - size // 2:
            going_left = lax.ppermute(going_left, "tile", to_left)
            ahead.append(going_left)
    by_offset = [back[0]] + ahead + [back[size - d] for d in range(len(ahead) + 1, size)]
    order = (jnp.arange(size, dtype=jnp.int32) - me) % size
    return jnp.stack(by_offset)[order]


def reduce_probe(probe_part, owners, layers):
    piece_len = probe_part.size // owners
    pieces = probe_part.reshape(owners, piece_len)
    mine = jnp.sum(lax.all_to_all(pieces, "pos", 0, 0, tiled=True), axis=0)
    spread = jnp.broadcast_to(mine[None], (layers, piece_len))
    mine = jnp.sum(lax.all_to_all(spread, "tile", 0, 0, tiled=True), axis=0)
    spread = jnp.broadcast_to(mine[None], (owners, piece_len))
    gathered = lax.all_to_all(spread, "pos", 0, 0, tiled=True)
    return gathered.reshape(probe_part.shape)


def solution(mesh):
    in_specs = (P("pos", None, None), P(), P(), P(), P(("pos", "tile"), None, None))
    out_specs = (P("pos", None, None), P())
    return jax.shard_map(
        per_device, mesh=mesh, in_specs=in_specs, out_specs=out_specs, check_vma=False
    )
```
